512 devices in a mesh: band: 32 (over z, x), lev: 16 (over y, core).
Axes of the slice: x: 4, y: 8, z: 8, core: 2. Of those that a mesh axis runs over, the one named last changes fastest.
Arguments:
- spectral: bfloat16 [4, 128, 640, 640], P(None, 'lev', 'band'), may hold values from -6 to 6
- legendre_value: bfloat16 [640, 32, 640], P('band'), may hold values from -0.009765625 to 0.009765625
- legendre_slope: bfloat16 [640, 32, 640], P('band'), may hold values from -0.009765625 to 0.009765625
- wave_numbers: int32 [640], replicated, may hold values from 0 to 639, each once
- aerosol_old: bfloat16 [40, 128, 32, 2688], P(None, 'lev', 'band'), may hold values from 0 to 2
- vertical_weight: bfloat16 [3, 128, 32, 2688], P(None, 'lev', 'band'), may hold values from 0 to 0.59765625
- send_blocks: int32 [32, 5, 4], P('band'), may hold values from -1 to 20, as said below
- depart_slot: int32 [672, 4], P('band'), may hold values from 0 to 19, as said below
- depart_offset: int32 [672, 4, 128], P('band'), may hold values from 0 to 124
- depart_weight: bfloat16 [672, 4, 4, 128], P('band'), may hold values from 0 to 0.5
Outputs:
- wind_grid: bfloat16 [2, 128, 32, 2688], P(None, 'lev', 'band')
- aerosol_new: bfloat16 [40, 128, 32, 2688], P(None, 'lev', 'band')
- aerosol_flux: bfloat16 [2, 128, 32, 2688], P(None, 'lev', 'band')
The draws below stay inside these ranges and needn't reach their ends.
Inputs may be any that keep to these rules, and one draw needn't show every extreme that they name: `send_blocks`: row b, offset o lists up to 4 of band b's own blocks (block l * 21 + c is the band's latitude l, longitudes c * 128 onward) that band b + o - 2 reads; -1 marks an empty slot; offsets toward bands that do not exist are empty; some rows are full. `depart_slot`: slot o * 4 + e of band r's pool is what band r - o + 2 lists at offset o, slot e; arrival block g belongs to band g // 21 and every slot it names is filled.
All inputs are finite; a program needn't handle non-finite values.
Results may differ from the reference program's by a relative error of at most 0.0062.
Values may be sent and summed in bfloat16 or wider, within the bound.
No kernel may reach another device: no remote copies, remote signals or barrier semaphores. Data moves between devices by JAX's collectives and lax.ppermute only.
A program may use at most 128 MiB of HBM per device.

```python
import math
import jax
import jax.numpy as jnp
from jax import lax

WAVES = 640
TRUNC = 640
BINS = 40
NLON = 2688
BLK = 128
STENCIL = 4
REACH = 2
CAP = 4
LAT_DEV = 1
LEVELS = 128
NLAT = 32
NBL = 21
NB = 21
NBLK = 672
OFFS = 5


def routing_tables(key):
    band_count = NLAT // LAT_DEV
    count_key = jax.random.fold_in(key, 101)
    block_key = jax.random.fold_in(key, 202)
    pick_key = jax.random.fold_in(key, 303)
    band_rows = jnp.arange(band_count, dtype=jnp.int32)[:, None]
    offsets = jnp.arange(OFFS, dtype=jnp.int32)[None, :]
    targets = band_rows + offsets - REACH
    inside = (targets >= 0) & (targets < band_count)
    near_pole = (band_rows <= 2 * REACH) | (band_rows >= band_count - 1 - 2 * REACH)
    counts = jax.random.randint(count_key, (band_count, OFFS), 1, CAP + 1)
    counts = jnp.where(near_pole, CAP, counts)
    counts = jnp.where(inside, counts, 0)
    slot_number = jnp.arange(CAP, dtype=jnp.int32)
    filled = slot_number[None, None, :] < counts[:, :, None]
    chosen = jax.random.randint(block_key, (band_count, OFFS, CAP), 0, NB)
    chosen = chosen.at[:, REACH, 0].set(NB - 1)
    listed = jnp.where(filled, chosen, -1)
    senders = band_rows - offsets + REACH
    sender_valid = (senders >= 0) & (senders < band_count)
    pool_filled = filled[jnp.clip(senders, 0, band_count - 1), offsets] & sender_valid[:, :, None]
    pool_filled = pool_filled.reshape(band_count, OFFS * CAP).astype(jnp.int32)
    live_count = jnp.sum(pool_filled, axis=1)
    slot_ranks = jnp.cumsum(pool_filled, axis=1) - 1
    random_bits = jax.random.randint(pick_key, (band_count, NB, STENCIL), 0, 1 << 20)
    wanted = random_bits % live_count[:, None, None]
    wanted = wanted.at[:, 0, 0].set(live_count - 1)
    wanted = wanted.at[:, 0, 1].set(0)
    matches = (slot_ranks[:, None, None, :] == wanted[:, :, :, None]) & (pool_filled[:, None, None, :] == 1)
    picked = jnp.argmax(matches.astype(jnp.int32), axis=-1).astype(jnp.int32)
    return (listed.astype(jnp.int32), picked.reshape(band_count * NB, STENCIL))


def draw_send_blocks(key, part):
    listed, picked = routing_tables(key)
    return listed


def draw_depart_slot(key, part):
    listed, picked = routing_tables(key)
    return picked


def set_ends(array, own_key, smallest, top_value):
    longest = array.shape.index(max(array.shape))
    spots = []
    for shift in (0, 1):
        where = [jax.random.randint(jax.random.fold_in(own_key, axis), (), 0, length) for axis, length in enumerate(array.shape)]
        where[longest] = (where[longest] + shift) % array.shape[longest]
        spots.append(tuple(where))
    return array.at[spots[0]].set(smallest).at[spots[1]].set(top_value)


def steps_of(key, shape, split, smallest, top_value):
    def one(axis_at, shards_of):
        steps = jax.random.uniform(jax.random.fold_in(jax.random.fold_in(key, 6), axis_at), (shards_of,), jnp.float32, smallest / len(split), top_value / len(split))
        return jnp.repeat(jnp.exp(steps), shape[axis_at] // shards_of).reshape((-1,) + (1,) * (len(shape) - axis_at - 1))

    gain = one(*split[0])
    for cut in split[1:]:
        gain = gain * one(*cut)
    return gain


def scatter_about(key, dims, scale, reach, shards=(), held_as=jnp.bfloat16):
    entries = jax.random.normal(key, dims, jnp.float32) * scale
    if len(shards) > 0:
        entries = steps_of(key, dims, shards, -0.22, 0.18) * entries
    return jnp.clip(entries, min=-reach, max=reach).astype(held_as)


def setup_inputs(seed: int = 0) -> dict:
    key_of = jax.random.split(jax.random.key(seed), 11)
    spectral = scatter_about(key_of[0], (4, LEVELS, WAVES, TRUNC), 1.0, 6.0, ((1, 16), (2, 32)))
    legendre_value = scatter_about(key_of[1], (WAVES, NLAT, TRUNC), (TRUNC * WAVES) ** -0.5, 0.009765625, ((0, 32),))
    legendre_slope = scatter_about(key_of[2], (WAVES, NLAT, TRUNC), (TRUNC * WAVES) ** -0.5, 0.009765625, ((0, 32),))
    wave_numbers = jax.random.permutation(key_of[3], WAVES).astype(jnp.int32)
    aerosol_old = jnp.clip(2.0 * jax.random.uniform(key_of[4], (BINS, LEVELS, NLAT, NLON), jnp.float32) ** steps_of(key_of[4], (BINS, LEVELS, NLAT, NLON), ((1, 16), (2, 32)), -0.2, 0.2), 0.0, 2.0).astype(jnp.bfloat16)
    vertical_weight = jnp.clip(0.59765625 * jax.random.uniform(key_of[5], (3, LEVELS, NLAT, NLON), jnp.float32) ** steps_of(key_of[5], (3, LEVELS, NLAT, NLON), ((1, 16), (2, 32)), -0.2, 0.2), 0.0, 0.59765625).astype(jnp.bfloat16)
    send_blocks = draw_send_blocks(jax.random.fold_in(key_of[10], 71), 0)
    depart_slot = draw_depart_slot(jax.random.fold_in(key_of[10], 71), 0)
    depart_offset = set_ends(jax.random.randint(key_of[8], (NBLK, STENCIL, BLK), 0, BLK - STENCIL + 1), jax.random.fold_in(key_of[8], 1), 0, BLK - STENCIL).astype(jnp.int32)
    depart_weight = jnp.clip(0.5 * jax.random.uniform(key_of[9], (NBLK, STENCIL, STENCIL, BLK), jnp.float32) ** steps_of(key_of[9], (NBLK, STENCIL, STENCIL, BLK), ((0, 32),), -0.2, 0.2), 0.0, 0.5).astype(jnp.bfloat16)
    return {"spectral": spectral, "legendre_value": legendre_value, "legendre_slope": legendre_slope, "wave_numbers": wave_numbers, "aerosol_old": aerosol_old, "vertical_weight": vertical_weight, "send_blocks": send_blocks, "depart_slot": depart_slot, "depart_offset": depart_offset, "depart_weight": depart_weight}


def fourier_table(wave_numbers, lon_count):
    longitudes = jnp.arange(lon_count, dtype=jnp.int32)
    phases = (wave_numbers[:, None] * longitudes[None, :]) % lon_count
    angles = phases.astype(jnp.float32) * (2.0 * math.pi / lon_count)
    doubled = jnp.where(wave_numbers == 0, 1.0, 2.0).astype(jnp.float32)[:, None]
    return jnp.stack([doubled * jnp.cos(angles), -doubled * jnp.sin(angles)]).astype(jnp.bfloat16)


def stencil_matrix(depart_offset, depart_weight):
    width = depart_offset.shape[-1]
    columns = jnp.arange(width, dtype=jnp.int32)
    summed = jnp.zeros(depart_offset.shape[:2] + (width, width), jnp.float32)
    for term_index in range(depart_weight.shape[2]):
        matches = columns[None, None, :, None] == (depart_offset[:, :, None, :] + term_index)
        summed = summed + jnp.where(matches, depart_weight[:, :, term_index, None, :].astype(jnp.float32), 0.0)
    return summed


def reference(spectral, legendre_value, legendre_slope, wave_numbers, aerosol_old, vertical_weight, send_blocks, depart_slot, depart_offset, depart_weight):
    spectral_wide = spectral.astype(jnp.float32)
    value_terms = jnp.einsum('slj,xksj->xkls', legendre_value.astype(jnp.float32), spectral_wide)
    slope_terms = jnp.einsum('slj,xksj->xkls', legendre_slope.astype(jnp.float32), spectral_wide)
    factor = wave_numbers.astype(jnp.float32) / WAVES
    coefficients = jnp.stack([
        -slope_terms[0] - factor * value_terms[3],
        -slope_terms[1] + factor * value_terms[2],
        slope_terms[2] - factor * value_terms[1],
        slope_terms[3] + factor * value_terms[0]]).astype(jnp.bfloat16)
    fourier = fourier_table(wave_numbers, NLON)
    paired = coefficients.astype(jnp.float32).reshape(2, 2, LEVELS, NLAT, WAVES)
    wind_grid = jnp.einsum('wxklm,xmi->wkli', paired, fourier.astype(jnp.float32)).astype(jnp.bfloat16)

    weights = vertical_weight.astype(jnp.float32)

    def remap_bin(column):
        padded = jnp.pad(column.astype(jnp.float32), ((1, 1), (0, 0), (0, 0)))
        return (weights[0] * padded[:-2] + weights[1] * padded[1:-1] + weights[2] * padded[2:]).astype(jnp.bfloat16)

    remapped = lax.map(remap_bin, aerosol_old)
    blocks = remapped.reshape(BINS, LEVELS, NBLK, BLK).transpose(2, 0, 1, 3).reshape(NBLK, BINS * LEVELS, BLK)
    band_count = NLAT // LAT_DEV
    band_rows = jnp.arange(band_count, dtype=jnp.int32)[:, None]
    offsets = jnp.arange(OFFS, dtype=jnp.int32)[None, :]
    senders = jnp.clip(band_rows - offsets + REACH, 0, band_count - 1)
    listed = send_blocks[senders, offsets]
    global_ids = (senders[:, :, None] * NB + jnp.clip(listed, 0, NB - 1)).reshape(band_count, OFFS * CAP)
    owners = jnp.arange(NBLK, dtype=jnp.int32) // NB
    source_block = global_ids[owners[:, None], depart_slot]

    def one_band(inputs):
        sources, shifts, stencil_weights = inputs
        chosen = blocks[sources].astype(jnp.float32)
        stencil = stencil_matrix(shifts, stencil_weights)
        return jnp.einsum('jifq,jiqp->jfp', chosen, stencil).astype(jnp.bfloat16)

    results = lax.map(one_band, (source_block.reshape(band_count, NB, STENCIL),
                                 depart_offset.reshape(band_count, NB, STENCIL, BLK),
                                 depart_weight.reshape(band_count, NB, STENCIL, STENCIL, BLK)))
    aerosol_new = results.reshape(NLAT, NBL, BINS, LEVELS, BLK).transpose(2, 3, 0, 1, 4).reshape(BINS, LEVELS, NLAT, NLON)
    average = jnp.mean(aerosol_new.astype(jnp.float32), axis=0)
    aerosol_flux = (wind_grid.astype(jnp.float32) * average[None]).astype(jnp.bfloat16)
    return (wind_grid, aerosol_new, aerosol_flux)
```

```python
import math

import jax
import jax.numpy as jnp
from jax import lax
from jax.sharding import PartitionSpec as P

WAVES = 640
NLON = 2688
BLK = 128


def extended(cells, sides, width):
    for axis, dim in sides:
        count = lax.axis_size(axis)
        ends = count - 1
        head = lax.slice_in_dim(cells, 0, width, axis=dim)
        tail = lax.slice_in_dim(cells, cells.shape[dim] - width, cells.shape[dim], axis=dim)
        cells = jnp.concatenate(
            [
                lax.ppermute(tail, axis, [(i, (i + 1) % count) for i in range(ends)]),
                cells,
                lax.ppermute(head, axis, [((i + 1) % count, i) for i in range(ends)]),
            ],
            axis=dim,
        )
    return cells


def shifted(value, axis, steps):
    count = lax.axis_size(axis)
    leading, last = (max(0, -steps), min(count, count - steps))
    return lax.ppermute(value, axis, [(source, source + steps) for source in range(leading, last)])


def fourier_table(wave_numbers, lon_count):
    inner = BLK
    outer = lon_count // inner
    waves = wave_numbers[:, None]
    near = (waves * jnp.arange(inner, dtype=jnp.int32)[None, :]) % lon_count
    far = (waves * (jnp.arange(outer, dtype=jnp.int32) * inner)[None, :]) % lon_count
    scale = 2.0 * math.pi / lon_count
    near_angle = near.astype(jnp.float32) * scale
    far_angle = far.astype(jnp.float32) * scale
    near_cos = jnp.cos(near_angle)[:, None, :]
    near_sin = jnp.sin(near_angle)[:, None, :]
    far_cos = jnp.cos(far_angle)[:, :, None]
    far_sin = jnp.sin(far_angle)[:, :, None]
    cosine = (near_cos * far_cos - near_sin * far_sin).reshape(-1, lon_count)
    sine = (near_sin * far_cos + near_cos * far_sin).reshape(-1, lon_count)
    doubled = jnp.where(wave_numbers == 0, 1.0, 2.0).astype(jnp.float32)[:, None]
    return jnp.stack([doubled * cosine, -doubled * sine]).astype(jnp.bfloat16)


def stencil_matrix(depart_offset, depart_weight):
    width = depart_offset.shape[-1]
    columns = jnp.arange(width, dtype=jnp.int32)
    summed = jnp.zeros(depart_offset.shape[:2] + (width, width), jnp.float32)
    for term_index in range(depart_weight.shape[2]):
        matches = columns[None, None, :, None] == depart_offset[:, :, None, :] + term_index
        summed = summed + jnp.where(
            matches, depart_weight[:, :, term_index, None, :].astype(jnp.float32), 0.0
        )
    return summed


def shards(
    spectral,
    legendre_value,
    legendre_slope,
    wave_numbers,
    aerosol_old,
    vertical_weight,
    send_blocks,
    depart_slot,
    depart_offset,
    depart_weight,
):
    band_here = lax.axis_index("band")
    wave_local = spectral.shape[2]
    own_waves = lax.dynamic_slice_in_dim(wave_numbers, band_here * wave_local, wave_local, 0)
    value_terms = jnp.einsum(
        "slj,xksj->xkls", legendre_value, spectral, preferred_element_type=jnp.float32
    )
    slope_terms = jnp.einsum(
        "slj,xksj->xkls", legendre_slope, spectral, preferred_element_type=jnp.float32
    )
    factor = own_waves.astype(jnp.float32) / WAVES
    coefficients = jnp.stack(
        [
            -slope_terms[0] - factor * value_terms[3],
            -slope_terms[1] + factor * value_terms[2],
            slope_terms[2] - factor * value_terms[1],
            slope_terms[3] + factor * value_terms[0],
        ]
    ).astype(jnp.bfloat16)
    fourier = fourier_table(wave_numbers, NLON)
    received = lax.all_to_all(coefficients, "band", split_axis=2, concat_axis=3, tiled=True)
    paired = received.reshape(2, 2, received.shape[1], received.shape[2], received.shape[3])
    wind_grid = jnp.einsum(
        "wxklm,xmi->wkli", paired, fourier, preferred_element_type=jnp.float32
    ).astype(jnp.bfloat16)
    padded = extended(aerosol_old, (("lev", 1),), 1)
    weights = vertical_weight.astype(jnp.float32)
    vertical_sum = (
        weights[0] * padded[:, :-2] + weights[1] * padded[:, 1:-1] + weights[2] * padded[:, 2:]
    )
    remapped = vertical_sum.astype(jnp.bfloat16)
    bin_count, level_count, lat_count, lon_count = remapped.shape
    block_count = lon_count // BLK
    blocks = remapped.reshape(bin_count, level_count, lat_count, block_count, BLK).transpose(
        2, 3, 0, 1, 4
    )
    blocks = blocks.reshape(lat_count * block_count, bin_count * level_count, BLK)
    listed = send_blocks[0]
    outgoing = jnp.take(blocks, jnp.clip(listed, 0, blocks.shape[0] - 1), axis=0)
    stencil = stencil_matrix(depart_offset, depart_weight).astype(jnp.bfloat16)
    offsets = listed.shape[0]
    reach_bands = offsets // 2
    pieces = []
    for offset_index in range(offsets):
        shift_by = offset_index - reach_bands
        if shift_by == 0:
            pieces.append(outgoing[offset_index])
        else:
            pieces.append(shifted(outgoing[offset_index], "band", shift_by))
    pooled = jnp.stack(pieces)
    flattened = pooled.reshape(pooled.shape[0] * pooled.shape[1], pooled.shape[2], pooled.shape[3])
    chosen = jnp.take(flattened, depart_slot, axis=0)
    block_rows = jnp.einsum("jifq,jiqp->jfp", chosen, stencil, preferred_element_type=jnp.float32)
    aerosol_new = block_rows.reshape(lat_count, block_count, bin_count, level_count, BLK).transpose(
        2, 3, 0, 1, 4
    )
    aerosol_new = aerosol_new.reshape(bin_count, level_count, lat_count, lon_count).astype(
        jnp.bfloat16
    )
    average = jnp.mean(aerosol_new.astype(jnp.float32), axis=0)
    aerosol_flux = (wind_grid.astype(jnp.float32) * average[None]).astype(jnp.bfloat16)
    return (wind_grid, aerosol_new, aerosol_flux)


def solution(mesh):
    return jax.shard_map(
        shards,
        mesh=mesh,
        in_specs=(
            P(None, "lev", "band", None),
            P("band", None, None),
            P("band", None, None),
            P(),
            P(None, "lev", "band", None),
            P(None, "lev", "band", None),
            P("band", None, None),
            P("band", None),
            P("band", None, None),
            P("band", None, None, None),
        ),
        out_specs=(
            P(None, "lev", "band", None),
            P(None, "lev", "band", None),
            P(None, "lev", "band", None),
        ),
        check_vma=False,
    )
```

```python
import math

import jax
import jax.numpy as jnp
from jax import lax
from jax.sharding import PartitionSpec as P

WAVES = 640
NLON = 2688
BLK = 128


def extended(cells, sides, width):
    for axis, dim in sides:
        count = lax.axis_size(axis)
        ends = count - 1
        head = lax.slice_in_dim(cells, 0, width, axis=dim)
        tail = lax.slice_in_dim(cells, cells.shape[dim] - width, cells.shape[dim], axis=dim)
        cells = jnp.concatenate(
            [
                lax.ppermute(tail, axis, [(i, (i + 1) % count) for i in range(ends)]),
                cells,
                lax.ppermute(head, axis, [((i + 1) % count, i) for i in range(ends)]),
            ],
            axis=dim,
        )
    return cells


def shifted(value, axis, steps):
    count = lax.axis_size(axis)
    leading, last = (max(0, -steps), min(count, count - steps))
    return lax.ppermute(value, axis, [(source, source + steps) for source in range(leading, last)])


def synthesis(coefficients, wave_numbers, lon_count):
    inner = BLK
    outer = lon_count // inner
    waves = wave_numbers[:, None]
    scale = 2.0 * math.pi / lon_count
    near = (waves * jnp.arange(inner, dtype=jnp.int32)[None, :]) % lon_count
    far = (waves * (jnp.arange(outer, dtype=jnp.int32) * inner)[None, :]) % lon_count
    near_angle = near.astype(jnp.float32) * scale
    far_angle = far.astype(jnp.float32) * scale
    doubled = jnp.where(wave_numbers == 0, 1.0, 2.0).astype(jnp.float32)
    far_cos = (doubled[:, None] * jnp.cos(far_angle)).T
    far_sin = (doubled[:, None] * jnp.sin(far_angle)).T
    wide = coefficients.astype(jnp.float32)
    real = wide[0::2][..., None, :]
    imag = wide[1::2][..., None, :]
    first = real * far_cos - imag * far_sin
    second = -(real * far_sin + imag * far_cos)
    lhs = jnp.concatenate([first, second], axis=-1)
    rhs = jnp.concatenate([jnp.cos(near_angle), jnp.sin(near_angle)], axis=0)
    out = jnp.einsum("wklom,mi->wkloi", lhs, rhs, precision=lax.Precision.HIGHEST,
                     preferred_element_type=jnp.float32)
    return out.reshape(out.shape[:3] + (lon_count,))


def stencil_matrix(depart_offset, depart_weight):
    width = depart_offset.shape[-1]
    columns = jnp.arange(width, dtype=jnp.int32)
    summed = jnp.zeros(depart_offset.shape[:2] + (width, width), jnp.float32)
    for term_index in range(depart_weight.shape[2]):
        matches = columns[None, None, :, None] == depart_offset[:, :, None, :] + term_index
        summed = summed + jnp.where(
            matches, depart_weight[:, :, term_index, None, :].astype(jnp.float32), 0.0
        )
    return summed


def shards(
    spectral,
    legendre_value,
    legendre_slope,
    wave_numbers,
    aerosol_old,
    vertical_weight,
    send_blocks,
    depart_slot,
    depart_offset,
    depart_weight,
):
    band_here = lax.axis_index("band")
    wave_local = spectral.shape[2]
    own_waves = lax.dynamic_slice_in_dim(wave_numbers, band_here * wave_local, wave_local, 0)
    value_terms = jnp.einsum(
        "slj,xksj->xkls", legendre_value, spectral, preferred_element_type=jnp.float32
    )
    slope_terms = jnp.einsum(
        "slj,xksj->xkls", legendre_slope, spectral, preferred_element_type=jnp.float32
    )
    factor = own_waves.astype(jnp.float32) / WAVES
    coefficients = jnp.stack(
        [
            -slope_terms[0] - factor * value_terms[3],
            -slope_terms[1] + factor * value_terms[2],
            slope_terms[2] - factor * value_terms[1],
            slope_terms[3] + factor * value_terms[0],
        ]
    ).astype(jnp.bfloat16)
    received = lax.all_to_all(coefficients, "band", split_axis=2, concat_axis=3, tiled=True)
    wind_grid = synthesis(received, wave_numbers, NLON).astype(jnp.bfloat16)
    padded = extended(aerosol_old, (("lev", 1),), 1)
    weights = vertical_weight.astype(jnp.float32)
    vertical_sum = (
        weights[0] * padded[:, :-2] + weights[1] * padded[:, 1:-1] + weights[2] * padded[:, 2:]
    )
    remapped = vertical_sum.astype(jnp.bfloat16)
    bin_count, level_count, lat_count, lon_count = remapped.shape
    block_count = lon_count // BLK
    blocks = remapped.reshape(bin_count, level_count, lat_count, block_count, BLK).transpose(
        2, 3, 0, 1, 4
    )
    blocks = blocks.reshape(lat_count * block_count, bin_count * level_count, BLK)
    listed = send_blocks[0]
    outgoing = jnp.take(blocks, jnp.clip(listed, 0, blocks.shape[0] - 1), axis=0)
    stencil = stencil_matrix(depart_offset, depart_weight).astype(jnp.bfloat16)
    offsets = listed.shape[0]
    reach_bands = offsets // 2
    pieces = []
    for offset_index in range(offsets):
        shift_by = offset_index - reach_bands
        if shift_by == 0:
            pieces.append(outgoing[offset_index])
        else:
            pieces.append(shifted(outgoing[offset_index], "band", shift_by))
    pooled = jnp.stack(pieces)
    flattened = pooled.reshape(pooled.shape[0] * pooled.shape[1], pooled.shape[2], pooled.shape[3])
    chosen = jnp.take(flattened, depart_slot, axis=0)
    block_rows = jnp.einsum("jifq,jiqp->jfp", chosen, stencil, preferred_element_type=jnp.float32)
    aerosol_new = block_rows.reshape(lat_count, block_count, bin_count, level_count, BLK).transpose(
        2, 3, 0, 1, 4
    )
    aerosol_new = aerosol_new.reshape(bin_count, level_count, lat_count, lon_count).astype(
        jnp.bfloat16
    )
    average = jnp.mean(aerosol_new.astype(jnp.float32), axis=0)
    aerosol_flux = (wind_grid.astype(jnp.float32) * average[None]).astype(jnp.bfloat16)
    return (wind_grid, aerosol_new, aerosol_flux)


def solution(mesh):
    return jax.shard_map(
        shards,
        mesh=mesh,
        in_specs=(
            P(None, "lev", "band", None),
            P("band", None, None),
            P("band", None, None),
            P(),
            P(None, "lev", "band", None),
            P(None, "lev", "band", None),
            P("band", None, None),
            P("band", None),
            P("band", None, None),
            P("band", None, None, None),
        ),
        out_specs=(
            P(None, "lev", "band", None),
            P(None, "lev", "band", None),
            P(None, "lev", "band", None),
        ),
        check_vma=False,
    )
```

```python
import math

import jax
import jax.numpy as jnp
from jax import lax
from jax.experimental import pallas as pl
from jax.experimental.pallas import tpu as pltpu
from jax.sharding import PartitionSpec as P

WAVES = 640
NLON = 2688
BLK = 128


def extended(cells, sides, width):
    for axis, dim in sides:
        count = lax.axis_size(axis)
        ends = count - 1
        head = lax.slice_in_dim(cells, 0, width, axis=dim)
        tail = lax.slice_in_dim(cells, cells.shape[dim] - width, cells.shape[dim], axis=dim)
        cells = jnp.concatenate(
            [
                lax.ppermute(tail, axis, [(i, (i + 1) % count) for i in range(ends)]),
                cells,
                lax.ppermute(head, axis, [((i + 1) % count, i) for i in range(ends)]),
            ],
            axis=dim,
        )
    return cells


def shifted(value, axis, steps):
    count = lax.axis_size(axis)
    leading, last = (max(0, -steps), min(count, count - steps))
    return lax.ppermute(value, axis, [(source, source + steps) for source in range(leading, last)])


def synthesis(coefficients, wave_numbers, lon_count):
    inner = BLK
    outer = lon_count // inner
    waves = wave_numbers[:, None]
    scale = 2.0 * math.pi / lon_count
    near = (waves * jnp.arange(inner, dtype=jnp.int32)[None, :]) % lon_count
    far = (waves * (jnp.arange(outer, dtype=jnp.int32) * inner)[None, :]) % lon_count
    near_angle = near.astype(jnp.float32) * scale
    far_angle = far.astype(jnp.float32) * scale
    doubled = jnp.where(wave_numbers == 0, 1.0, 2.0).astype(jnp.float32)
    far_cos = (doubled[:, None] * jnp.cos(far_angle)).T
    far_sin = (doubled[:, None] * jnp.sin(far_angle)).T
    wide = coefficients.astype(jnp.float32)
    real = wide[0::2][..., None, :]
    imag = wide[1::2][..., None, :]
    first = real * far_cos - imag * far_sin
    second = -(real * far_sin + imag * far_cos)
    lhs = jnp.concatenate([first, second], axis=-1)
    rhs = jnp.concatenate([jnp.cos(near_angle), jnp.sin(near_angle)], axis=0)
    out = jnp.einsum("wklom,mi->wkloi", lhs, rhs, precision=lax.Precision.HIGHEST,
                     preferred_element_type=jnp.float32)
    return out.reshape(out.shape[:3] + (lon_count,))


def stencil_matrix(depart_offset, depart_weight):
    width = depart_offset.shape[-1]
    columns = jnp.arange(width, dtype=jnp.int32)
    summed = jnp.zeros(depart_offset.shape[:2] + (width, width), jnp.float32)
    for term_index in range(depart_weight.shape[2]):
        matches = columns[None, None, :, None] == depart_offset[:, :, None, :] + term_index
        summed = summed + jnp.where(
            matches, depart_weight[:, :, term_index, None, :].astype(jnp.float32), 0.0
        )
    return summed


def pack_blocks(listed, remapped, offsets, cap):
    rows = remapped.shape[0]

    def body(listed_ref, *refs):
        for index in range(offsets):
            refs[offsets + index][...] = refs[index][...][None]

    def source_map(index):
        return lambda entry, table: (0, table[index * cap + entry])

    out_shape = [jax.ShapeDtypeStruct((cap, rows, BLK), remapped.dtype) for _ in range(offsets)]
    grid_spec = pltpu.PrefetchScalarGridSpec(
        num_scalar_prefetch=1,
        grid=(cap,),
        in_specs=[pl.BlockSpec((rows, BLK), source_map(index)) for index in range(offsets)],
        out_specs=[pl.BlockSpec((1, rows, BLK), lambda entry, table: (entry, 0, 0))
                   for _ in range(offsets)],
    )
    return pl.pallas_call(body, grid_spec=grid_spec, out_shape=out_shape)(
        listed, *([remapped] * offsets))


def apply_stencil(slots, stencil, pieces, bin_count, level_count):
    block_count, rows_per_block = stencil.shape[0], stencil.shape[1]
    count = len(pieces)
    cap, rows, _ = pieces[0].shape

    def body(slot_ref, stencil_ref, *refs):
        piece_refs = refs[:count]
        out_ref, mean_ref, acc_ref = refs[count:]
        block = pl.program_id(0)
        acc_ref[...] = jnp.zeros_like(acc_ref)
        for row in range(rows_per_block):
            slot = slot_ref[block * rows_per_block + row]
            piece = slot // cap
            entry = slot % cap
            weights = stencil_ref[0, row]
            for index in range(count):
                @pl.when(piece == index)
                def _(index=index):
                    acc_ref[...] += jnp.dot(piece_refs[index][entry], weights,
                                            preferred_element_type=jnp.float32)
        result = acc_ref[...].astype(out_ref.dtype)
        out_ref[...] = result
        summed = result.astype(jnp.float32).reshape(bin_count, level_count, BLK).sum(axis=0)
        mean_ref[...] = summed / bin_count

    grid_spec = pltpu.PrefetchScalarGridSpec(
        num_scalar_prefetch=1,
        grid=(block_count,),
        in_specs=[pl.BlockSpec((1, rows_per_block, BLK, BLK), lambda b, table: (b, 0, 0, 0))]
        + [pl.BlockSpec((cap, rows, BLK), lambda b, table: (0, 0, 0)) for _ in range(count)],
        out_specs=[pl.BlockSpec((rows, BLK), lambda b, table: (0, b)),
                   pl.BlockSpec((level_count, BLK), lambda b, table: (0, b))],
        scratch_shapes=[pltpu.VMEM((rows, BLK), jnp.float32)],
    )
    out_shape = [jax.ShapeDtypeStruct((rows, block_count * BLK), pieces[0].dtype),
                 jax.ShapeDtypeStruct((level_count, block_count * BLK), jnp.float32)]
    return pl.pallas_call(body, grid_spec=grid_spec, out_shape=out_shape)(slots, stencil, *pieces)


def shards(
    spectral,
    legendre_value,
    legendre_slope,
    wave_numbers,
    aerosol_old,
    vertical_weight,
    send_blocks,
    depart_slot,
    depart_offset,
    depart_weight,
):
    band_here = lax.axis_index("band")
    wave_local = spectral.shape[2]
    own_waves = lax.dynamic_slice_in_dim(wave_numbers, band_here * wave_local, wave_local, 0)
    value_terms = jnp.einsum(
        "slj,xksj->xkls", legendre_value, spectral, preferred_element_type=jnp.float32
    )
    slope_terms = jnp.einsum(
        "slj,xksj->xkls", legendre_slope, spectral, preferred_element_type=jnp.float32
    )
    factor = own_waves.astype(jnp.float32) / WAVES
    coefficients = jnp.stack(
        [
            -slope_terms[0] - factor * value_terms[3],
            -slope_terms[1] + factor * value_terms[2],
            slope_terms[2] - factor * value_terms[1],
            slope_terms[3] + factor * value_terms[0],
        ]
    ).astype(jnp.bfloat16)
    received = lax.all_to_all(coefficients, "band", split_axis=2, concat_axis=3, tiled=True)
    wind_grid = synthesis(received, wave_numbers, NLON).astype(jnp.bfloat16)
    padded = extended(aerosol_old, (("lev", 1),), 1)
    weights = vertical_weight.astype(jnp.float32)
    vertical_sum = (
        weights[0] * padded[:, :-2] + weights[1] * padded[:, 1:-1] + weights[2] * padded[:, 2:]
    )
    bin_count, level_count, lat_count, lon_count = aerosol_old.shape
    rows = bin_count * level_count
    remapped = vertical_sum.astype(jnp.bfloat16).reshape(rows, lat_count * lon_count)
    block_total = lat_count * lon_count // BLK
    listed = jnp.clip(send_blocks[0], 0, block_total - 1)
    offsets, cap = listed.shape
    outgoing = pack_blocks(listed.reshape(-1), remapped, offsets, cap)
    stencil = stencil_matrix(depart_offset, depart_weight).astype(jnp.bfloat16)
    reach_bands = offsets // 2
    pieces = []
    for offset_index in range(offsets):
        shift_by = offset_index - reach_bands
        if shift_by == 0:
            pieces.append(outgoing[offset_index])
        else:
            pieces.append(shifted(outgoing[offset_index], "band", shift_by))
    flat_new, average = apply_stencil(depart_slot.reshape(-1), stencil, pieces, bin_count, level_count)
    aerosol_new = flat_new.reshape(bin_count, level_count, lat_count, lon_count)
    average = average.reshape(level_count, lat_count, lon_count)
    aerosol_flux = (wind_grid.astype(jnp.float32) * average[None]).astype(jnp.bfloat16)
    return (wind_grid, aerosol_new, aerosol_flux)


def solution(mesh):
    return jax.shard_map(
        shards,
        mesh=mesh,
        in_specs=(
            P(None, "lev", "band", None),
            P("band", None, None),
            P("band", None, None),
            P(),
            P(None, "lev", "band", None),
            P(None, "lev", "band", None),
            P("band", None, None),
            P("band", None),
            P("band", None, None),
            P("band", None, None, None),
        ),
        out_specs=(
            P(None, "lev", "band", None),
            P(None, "lev", "band", None),
            P(None, "lev", "band", None),
        ),
        check_vma=False,
    )
```

```python
import math

import jax
import jax.numpy as jnp
from jax import lax
from jax.experimental import pallas as pl
from jax.experimental.pallas import tpu as pltpu
from jax.sharding import PartitionSpec as P

WAVES = 640
NLON = 2688
BLK = 128


def extended(cells, sides, width):
    for axis, dim in sides:
        count = lax.axis_size(axis)
        ends = count - 1
        head = lax.slice_in_dim(cells, 0, width, axis=dim)
        tail = lax.slice_in_dim(cells, cells.shape[dim] - width, cells.shape[dim], axis=dim)
        cells = jnp.concatenate(
            [
                lax.ppermute(tail, axis, [(i, (i + 1) % count) for i in range(ends)]),
                cells,
                lax.ppermute(head, axis, [((i + 1) % count, i) for i in range(ends)]),
            ],
            axis=dim,
        )
    return cells


def shifted(value, axis, steps):
    count = lax.axis_size(axis)
    leading, last = (max(0, -steps), min(count, count - steps))
    return lax.ppermute(value, axis, [(source, source + steps) for source in range(leading, last)])


def synthesis(coefficients, wave_numbers, lon_count):
    inner = BLK
    outer = lon_count // inner
    waves = wave_numbers[:, None]
    scale = 2.0 * math.pi / lon_count
    near = (waves * jnp.arange(inner, dtype=jnp.int32)[None, :]) % lon_count
    far = (waves * (jnp.arange(outer, dtype=jnp.int32) * inner)[None, :]) % lon_count
    near_angle = near.astype(jnp.float32) * scale
    far_angle = far.astype(jnp.float32) * scale
    doubled = jnp.where(wave_numbers == 0, 1.0, 2.0).astype(jnp.float32)
    far_cos = (doubled[:, None] * jnp.cos(far_angle)).T
    far_sin = (doubled[:, None] * jnp.sin(far_angle)).T
    wide = coefficients.astype(jnp.float32)
    real = wide[0::2][..., None, :]
    imag = wide[1::2][..., None, :]
    first = real * far_cos - imag * far_sin
    second = -(real * far_sin + imag * far_cos)
    lhs = jnp.concatenate([first, second], axis=-1)
    rhs = jnp.concatenate([jnp.cos(near_angle), jnp.sin(near_angle)], axis=0)
    out = jnp.einsum("wklom,mi->wkloi", lhs, rhs, precision=lax.Precision.HIGHEST,
                     preferred_element_type=jnp.float32)
    return out.reshape(out.shape[:3] + (lon_count,))


def stencil_matrix(depart_offset, depart_weight):
    width = depart_offset.shape[-1]
    columns = jnp.arange(width, dtype=jnp.int32)
    summed = jnp.zeros(depart_offset.shape[:2] + (width, width), jnp.float32)
    for term_index in range(depart_weight.shape[2]):
        matches = columns[None, None, :, None] == depart_offset[:, :, None, :] + term_index
        summed = summed + jnp.where(
            matches, depart_weight[:, :, term_index, None, :].astype(jnp.float32), 0.0
        )
    return summed


def pack_blocks(listed, remapped, offsets, cap):
    rows = remapped.shape[0]

    def body(listed_ref, source_ref, *refs):
        out_refs = refs[:offsets]
        sems = refs[offsets]
        copies = []
        for index in range(offsets):
            for entry in range(cap):
                column = pl.multiple_of(listed_ref[index * cap + entry] * BLK, BLK)
                copy = pltpu.make_async_copy(
                    source_ref.at[:, pl.ds(column, BLK)],
                    out_refs[index].at[entry],
                    sems.at[index * cap + entry],
                )
                copy.start()
                copies.append(copy)
        for copy in copies:
            copy.wait()

    out_shape = [jax.ShapeDtypeStruct((cap, rows, BLK), remapped.dtype) for _ in range(offsets)]
    grid_spec = pltpu.PrefetchScalarGridSpec(
        num_scalar_prefetch=1,
        grid=(1,),
        in_specs=[pl.BlockSpec(memory_space=pl.ANY)],
        out_specs=[pl.BlockSpec(memory_space=pl.ANY) for _ in range(offsets)],
        scratch_shapes=[pltpu.SemaphoreType.DMA((offsets * cap,))],
    )
    return pl.pallas_call(body, grid_spec=grid_spec, out_shape=out_shape)(listed, remapped)


def apply_stencil(slots, stencil, pieces, bin_count, level_count):
    block_count, rows_per_block = stencil.shape[0], stencil.shape[1]
    count = len(pieces)
    cap, rows, _ = pieces[0].shape

    def body(slot_ref, stencil_ref, *refs):
        piece_refs = refs[:count]
        out_ref, mean_ref, pool_ref, sems = refs[count:]
        block = pl.program_id(0)

        @pl.when(block == 0)
        def _():
            copies = [pltpu.make_async_copy(piece_refs[index], pool_ref.at[pl.ds(index * cap, cap)],
                                            sems.at[index]) for index in range(count)]
            for copy in copies:
                copy.start()
            for copy in copies:
                copy.wait()

        total = None
        for row in range(rows_per_block):
            slot = jnp.clip(slot_ref[block * rows_per_block + row], 0, count * cap - 1)
            term = jnp.dot(pool_ref[slot], stencil_ref[0, row], preferred_element_type=jnp.float32)
            total = term if total is None else total + term
        result = total.astype(out_ref.dtype)
        out_ref[...] = result
        summed = result.astype(jnp.float32).reshape(bin_count, level_count, BLK).sum(axis=0)
        mean_ref[...] = summed / bin_count

    grid_spec = pltpu.PrefetchScalarGridSpec(
        num_scalar_prefetch=1,
        grid=(block_count,),
        in_specs=[pl.BlockSpec((1, rows_per_block, BLK, BLK), lambda b, table: (b, 0, 0, 0))]
        + [pl.BlockSpec(memory_space=pl.ANY) for _ in range(count)],
        out_specs=[pl.BlockSpec((rows, BLK), lambda b, table: (0, b)),
                   pl.BlockSpec((level_count, BLK), lambda b, table: (0, b))],
        scratch_shapes=[pltpu.VMEM((count * cap, rows, BLK), pieces[0].dtype),
                        pltpu.SemaphoreType.DMA((count,))],
    )
    out_shape = [jax.ShapeDtypeStruct((rows, block_count * BLK), pieces[0].dtype),
                 jax.ShapeDtypeStruct((level_count, block_count * BLK), jnp.float32)]
    return pl.pallas_call(
        body, grid_spec=grid_spec, out_shape=out_shape,
        compiler_params=pltpu.CompilerParams(dimension_semantics=("arbitrary",)),
    )(slots, stencil, *pieces)


def shards(
    spectral,
    legendre_value,
    legendre_slope,
    wave_numbers,
    aerosol_old,
    vertical_weight,
    send_blocks,
    depart_slot,
    depart_offset,
    depart_weight,
):
    band_here = lax.axis_index("band")
    wave_local = spectral.shape[2]
    own_waves = lax.dynamic_slice_in_dim(wave_numbers, band_here * wave_local, wave_local, 0)
    value_terms = jnp.einsum(
        "slj,xksj->xkls", legendre_value, spectral, preferred_element_type=jnp.float32
    )
    slope_terms = jnp.einsum(
        "slj,xksj->xkls", legendre_slope, spectral, preferred_element_type=jnp.float32
    )
    factor = own_waves.astype(jnp.float32) / WAVES
    coefficients = jnp.stack(
        [
            -slope_terms[0] - factor * value_terms[3],
            -slope_terms[1] + factor * value_terms[2],
            slope_terms[2] - factor * value_terms[1],
            slope_terms[3] + factor * value_terms[0],
        ]
    ).astype(jnp.bfloat16)
    received = lax.all_to_all(coefficients, "band", split_axis=2, concat_axis=3, tiled=True)
    wind_grid = synthesis(received, wave_numbers, NLON).astype(jnp.bfloat16)
    padded = extended(aerosol_old, (("lev", 1),), 1)
    weights = vertical_weight.astype(jnp.float32)
    vertical_sum = (
        weights[0] * padded[:, :-2] + weights[1] * padded[:, 1:-1] + weights[2] * padded[:, 2:]
    )
    bin_count, level_count, lat_count, lon_count = aerosol_old.shape
    rows = bin_count * level_count
    remapped = vertical_sum.astype(jnp.bfloat16).reshape(rows, lat_count * lon_count)
    block_total = lat_count * lon_count // BLK
    listed = jnp.clip(send_blocks[0], 0, block_total - 1)
    offsets, cap = listed.shape
    outgoing = pack_blocks(listed.reshape(-1), remapped, offsets, cap)
    stencil = stencil_matrix(depart_offset, depart_weight).astype(jnp.bfloat16)
    reach_bands = offsets // 2
    pieces = []
    for offset_index in range(offsets):
        shift_by = offset_index - reach_bands
        if shift_by == 0:
            pieces.append(outgoing[offset_index])
        else:
            pieces.append(shifted(outgoing[offset_index], "band", shift_by))
    flat_new, average = apply_stencil(depart_slot.reshape(-1), stencil, pieces, bin_count, level_count)
    aerosol_new = flat_new.reshape(bin_count, level_count, lat_count, lon_count)
    average = average.reshape(level_count, lat_count, lon_count)
    aerosol_flux = (wind_grid.astype(jnp.float32) * average[None]).astype(jnp.bfloat16)
    return (wind_grid, aerosol_new, aerosol_flux)


def solution(mesh):
    return jax.shard_map(
        shards,
        mesh=mesh,
        in_specs=(
            P(None, "lev", "band", None),
            P("band", None, None),
            P("band", None, None),
            P(),
            P(None, "lev", "band", None),
            P(None, "lev", "band", None),
            P("band", None, None),
            P("band", None),
            P("band", None, None),
            P("band", None, None, None),
        ),
        out_specs=(
            P(None, "lev", "band", None),
            P(None, "lev", "band", None),
            P(None, "lev", "band", None),
        ),
        check_vma=False,
    )
```

```python
import math

import jax
import jax.numpy as jnp
from jax import lax
from jax.experimental import pallas as pl
from jax.experimental.pallas import tpu as pltpu
from jax.sharding import PartitionSpec as P

WAVES = 640
NLON = 2688
BLK = 128


def extended(cells, sides, width):
    for axis, dim in sides:
        count = lax.axis_size(axis)
        ends = count - 1
        head = lax.slice_in_dim(cells, 0, width, axis=dim)
        tail = lax.slice_in_dim(cells, cells.shape[dim] - width, cells.shape[dim], axis=dim)
        cells = jnp.concatenate(
            [
                lax.ppermute(tail, axis, [(i, (i + 1) % count) for i in range(ends)]),
                cells,
                lax.ppermute(head, axis, [((i + 1) % count, i) for i in range(ends)]),
            ],
            axis=dim,
        )
    return cells


def shifted(value, axis, steps):
    count = lax.axis_size(axis)
    leading, last = (max(0, -steps), min(count, count - steps))
    return lax.ppermute(value, axis, [(source, source + steps) for source in range(leading, last)])


def synthesis(coefficients, wave_numbers, lon_count):
    inner = BLK
    outer = lon_count // inner
    waves = wave_numbers[:, None]
    scale = 2.0 * math.pi / lon_count
    near = (waves * jnp.arange(inner, dtype=jnp.int32)[None, :]) % lon_count
    far = (waves * (jnp.arange(outer, dtype=jnp.int32) * inner)[None, :]) % lon_count
    near_angle = near.astype(jnp.float32) * scale
    far_angle = far.astype(jnp.float32) * scale
    doubled = jnp.where(wave_numbers == 0, 1.0, 2.0).astype(jnp.float32)
    far_cos = (doubled[:, None] * jnp.cos(far_angle)).T
    far_sin = (doubled[:, None] * jnp.sin(far_angle)).T
    wide = coefficients.astype(jnp.float32)
    real = wide[0::2][..., None, :]
    imag = wide[1::2][..., None, :]
    first = real * far_cos - imag * far_sin
    second = -(real * far_sin + imag * far_cos)
    lhs = jnp.concatenate([first, second], axis=-1)
    rhs = jnp.concatenate([jnp.cos(near_angle), jnp.sin(near_angle)], axis=0)
    out = jnp.einsum("wklom,mi->wkloi", lhs, rhs, precision=lax.Precision.HIGHEST,
                     preferred_element_type=jnp.float32)
    return out.reshape(out.shape[:3] + (lon_count,))


def stencil_matrix(depart_offset, depart_weight):
    width = depart_offset.shape[-1]
    columns = jnp.arange(width, dtype=jnp.int32)
    summed = jnp.zeros(depart_offset.shape[:2] + (width, width), jnp.float32)
    for term_index in range(depart_weight.shape[2]):
        matches = columns[None, None, :, None] == depart_offset[:, :, None, :] + term_index
        summed = summed + jnp.where(
            matches, depart_weight[:, :, term_index, None, :].astype(jnp.float32), 0.0
        )
    return summed


def pack_blocks(listed, remapped, offsets, cap):
    rows = remapped.shape[0]

    def body(listed_ref, *refs):
        for index in range(offsets):
            refs[offsets + index][...] = refs[index][...][None]

    def source_map(index):
        return lambda entry, table: (0, table[index * cap + entry])

    out_shape = [jax.ShapeDtypeStruct((cap, rows, BLK), remapped.dtype) for _ in range(offsets)]
    grid_spec = pltpu.PrefetchScalarGridSpec(
        num_scalar_prefetch=1,
        grid=(cap,),
        in_specs=[pl.BlockSpec((rows, BLK), source_map(index)) for index in range(offsets)],
        out_specs=[pl.BlockSpec((1, rows, BLK), lambda entry, table: (entry, 0, 0))
                   for _ in range(offsets)],
    )
    return pl.pallas_call(body, grid_spec=grid_spec, out_shape=out_shape)(
        listed, *([remapped] * offsets))


def apply_stencil(slots, stencil, pieces, bin_count, level_count):
    block_count, rows_per_block = stencil.shape[0], stencil.shape[1]
    count = len(pieces)
    cap, rows, _ = pieces[0].shape

    def body(slot_ref, stencil_ref, *refs):
        piece_refs = refs[:count]
        out_ref, mean_ref, pool_ref, sems = refs[count:]
        block = pl.program_id(0)

        @pl.when(block == 0)
        def _():
            copies = [pltpu.make_async_copy(piece_refs[index], pool_ref.at[pl.ds(index * cap, cap)],
                                            sems.at[index]) for index in range(count)]
            for copy in copies:
                copy.start()
            for copy in copies:
                copy.wait()

        total = None
        for row in range(rows_per_block):
            slot = jnp.clip(slot_ref[block * rows_per_block + row], 0, count * cap - 1)
            term = jnp.dot(pool_ref[slot], stencil_ref[0, row], preferred_element_type=jnp.float32)
            total = term if total is None else total + term
        result = total.astype(out_ref.dtype)
        out_ref[...] = result
        summed = result.astype(jnp.float32).reshape(bin_count, level_count, BLK).sum(axis=0)
        mean_ref[...] = summed / bin_count

    grid_spec = pltpu.PrefetchScalarGridSpec(
        num_scalar_prefetch=1,
        grid=(block_count,),
        in_specs=[pl.BlockSpec((1, rows_per_block, BLK, BLK), lambda b, table: (b, 0, 0, 0))]
        + [pl.BlockSpec(memory_space=pl.ANY) for _ in range(count)],
        out_specs=[pl.BlockSpec((rows, BLK), lambda b, table: (0, b)),
                   pl.BlockSpec((level_count, BLK), lambda b, table: (0, b))],
        scratch_shapes=[pltpu.VMEM((count * cap, rows, BLK), pieces[0].dtype),
                        pltpu.SemaphoreType.DMA((count,))],
    )
    out_shape = [jax.ShapeDtypeStruct((rows, block_count * BLK), pieces[0].dtype),
                 jax.ShapeDtypeStruct((level_count, block_count * BLK), jnp.float32)]
    return pl.pallas_call(
        body, grid_spec=grid_spec, out_shape=out_shape,
        compiler_params=pltpu.CompilerParams(dimension_semantics=("arbitrary",)),
    )(slots, stencil, *pieces)


def shards(
    spectral,
    legendre_value,
    legendre_slope,
    wave_numbers,
    aerosol_old,
    vertical_weight,
    send_blocks,
    depart_slot,
    depart_offset,
    depart_weight,
):
    padded = extended(aerosol_old, (("lev", 1),), 1)
    weights = vertical_weight.astype(jnp.float32)
    vertical_sum = (
        weights[0] * padded[:, :-2] + weights[1] * padded[:, 1:-1] + weights[2] * padded[:, 2:]
    )
    bin_count, level_count, lat_count, lon_count = aerosol_old.shape
    rows = bin_count * level_count
    remapped = vertical_sum.astype(jnp.bfloat16).reshape(rows, lat_count * lon_count)
    block_total = lat_count * lon_count // BLK
    listed = jnp.clip(send_blocks[0], 0, block_total - 1)
    offsets, cap = listed.shape
    outgoing = pack_blocks(listed.reshape(-1), remapped, offsets, cap)
    outgoing, spectral, legendre_value, legendre_slope, depart_offset, depart_weight = (
        lax.optimization_barrier(
            (outgoing, spectral, legendre_value, legendre_slope, depart_offset, depart_weight)
        )
    )
    stencil = stencil_matrix(depart_offset, depart_weight).astype(jnp.bfloat16)
    reach_bands = offsets // 2
    pieces = []
    for offset_index in range(offsets):
        shift_by = offset_index - reach_bands
        if shift_by == 0:
            pieces.append(outgoing[offset_index])
        else:
            pieces.append(shifted(outgoing[offset_index], "band", shift_by))
    band_here = lax.axis_index("band")
    wave_local = spectral.shape[2]
    own_waves = lax.dynamic_slice_in_dim(wave_numbers, band_here * wave_local, wave_local, 0)
    value_terms = jnp.einsum(
        "slj,xksj->xkls", legendre_value, spectral, preferred_element_type=jnp.float32
    )
    slope_terms = jnp.einsum(
        "slj,xksj->xkls", legendre_slope, spectral, preferred_element_type=jnp.float32
    )
    factor = own_waves.astype(jnp.float32) / WAVES
    coefficients = jnp.stack(
        [
            -slope_terms[0] - factor * value_terms[3],
            -slope_terms[1] + factor * value_terms[2],
            slope_terms[2] - factor * value_terms[1],
            slope_terms[3] + factor * value_terms[0],
        ]
    ).astype(jnp.bfloat16)
    received = lax.all_to_all(coefficients, "band", split_axis=2, concat_axis=3, tiled=True)
    wind_grid = synthesis(received, wave_numbers, NLON).astype(jnp.bfloat16)
    pooled = jnp.stack(pieces)
    flattened = pooled.reshape(offsets * cap, rows, BLK)
    chosen = jnp.take(flattened, depart_slot, axis=0)
    block_rows = jnp.einsum("jifq,jiqp->jfp", chosen, stencil, preferred_element_type=jnp.float32)
    flat_new = block_rows.astype(jnp.bfloat16).transpose(1, 0, 2).reshape(rows, block_total * BLK)
    aerosol_new = flat_new.reshape(bin_count, level_count, lat_count, lon_count)
    average = jnp.mean(aerosol_new.astype(jnp.float32), axis=0)
    aerosol_flux = (wind_grid.astype(jnp.float32) * average[None]).astype(jnp.bfloat16)
    return (wind_grid, aerosol_new, aerosol_flux)


def solution(mesh):
    return jax.shard_map(
        shards,
        mesh=mesh,
        in_specs=(
            P(None, "lev", "band", None),
            P("band", None, None),
            P("band", None, None),
            P(),
            P(None, "lev", "band", None),
            P(None, "lev", "band", None),
            P("band", None, None),
            P("band", None),
            P("band", None, None),
            P("band", None, None, None),
        ),
        out_specs=(
            P(None, "lev", "band", None),
            P(None, "lev", "band", None),
            P(None, "lev", "band", None),
        ),
        check_vma=False,
    )
```

```python
import math

import jax
import jax.numpy as jnp
from jax import lax
from jax.experimental import pallas as pl
from jax.experimental.pallas import tpu as pltpu
from jax.sharding import PartitionSpec as P

WAVES = 640
NLON = 2688
BLK = 128


def extended(cells, sides, width):
    for axis, dim in sides:
        count = lax.axis_size(axis)
        ends = count - 1
        head = lax.slice_in_dim(cells, 0, width, axis=dim)
        tail = lax.slice_in_dim(cells, cells.shape[dim] - width, cells.shape[dim], axis=dim)
        cells = jnp.concatenate(
            [
                lax.ppermute(tail, axis, [(i, (i + 1) % count) for i in range(ends)]),
                cells,
                lax.ppermute(head, axis, [((i + 1) % count, i) for i in range(ends)]),
            ],
            axis=dim,
        )
    return cells


def shifted(value, axis, steps):
    count = lax.axis_size(axis)
    leading, last = (max(0, -steps), min(count, count - steps))
    return lax.ppermute(value, axis, [(source, source + steps) for source in range(leading, last)])


def synthesis(coefficients, wave_numbers, lon_count):
    inner = BLK
    outer = lon_count // inner
    waves = wave_numbers[:, None]
    scale = 2.0 * math.pi / lon_count
    near = (waves * jnp.arange(inner, dtype=jnp.int32)[None, :]) % lon_count
    far = (waves * (jnp.arange(outer, dtype=jnp.int32) * inner)[None, :]) % lon_count
    near_angle = near.astype(jnp.float32) * scale
    far_angle = far.astype(jnp.float32) * scale
    doubled = jnp.where(wave_numbers == 0, 1.0, 2.0).astype(jnp.float32)
    far_cos = (doubled[:, None] * jnp.cos(far_angle)).T
    far_sin = (doubled[:, None] * jnp.sin(far_angle)).T
    wide = coefficients.astype(jnp.float32)
    real = wide[0::2][..., None, :]
    imag = wide[1::2][..., None, :]
    first = real * far_cos - imag * far_sin
    second = -(real * far_sin + imag * far_cos)
    lhs = jnp.concatenate([first, second], axis=-1)
    rhs = jnp.concatenate([jnp.cos(near_angle), jnp.sin(near_angle)], axis=0)
    out = jnp.einsum("wklom,mi->wkloi", lhs, rhs, precision=lax.Precision.HIGHEST,
                     preferred_element_type=jnp.float32)
    return out.reshape(out.shape[:3] + (lon_count,))


def stencil_matrix(depart_offset, depart_weight):
    width = depart_offset.shape[-1]
    columns = jnp.arange(width, dtype=jnp.int32)
    summed = jnp.zeros(depart_offset.shape[:2] + (width, width), jnp.float32)
    for term_index in range(depart_weight.shape[2]):
        matches = columns[None, None, :, None] == depart_offset[:, :, None, :] + term_index
        summed = summed + jnp.where(
            matches, depart_weight[:, :, term_index, None, :].astype(jnp.float32), 0.0
        )
    return summed


def pack_blocks(listed, remapped, offsets, cap):
    rows = remapped.shape[0]

    def body(listed_ref, *refs):
        for index in range(offsets):
            refs[offsets + index][...] = refs[index][...][None]

    def source_map(index):
        return lambda entry, table: (0, table[index * cap + entry])

    out_shape = [jax.ShapeDtypeStruct((cap, rows, BLK), remapped.dtype) for _ in range(offsets)]
    grid_spec = pltpu.PrefetchScalarGridSpec(
        num_scalar_prefetch=1,
        grid=(cap,),
        in_specs=[pl.BlockSpec((rows, BLK), source_map(index)) for index in range(offsets)],
        out_specs=[pl.BlockSpec((1, rows, BLK), lambda entry, table: (entry, 0, 0))
                   for _ in range(offsets)],
    )
    return pl.pallas_call(body, grid_spec=grid_spec, out_shape=out_shape)(
        listed, *([remapped] * offsets))


def apply_stencil(slots, stencil, pieces, bin_count, level_count):
    block_count, rows_per_block = stencil.shape[0], stencil.shape[1]
    count = len(pieces)
    cap, rows, _ = pieces[0].shape
    group = 3 if block_count % 3 == 0 else 1

    def body(slot_ref, stencil_ref, *refs):
        piece_refs = refs[:count]
        out_ref, mean_ref, pool_ref, sems = refs[count:]
        block = pl.program_id(0)

        @pl.when(block == 0)
        def _():
            copies = [pltpu.make_async_copy(piece_refs[index], pool_ref.at[pl.ds(index * cap, cap)],
                                            sems.at[index]) for index in range(count)]
            for copy in copies:
                copy.start()
            for copy in copies:
                copy.wait()

        for member in range(group):
            total = None
            for row in range(rows_per_block):
                flat = (block * group + member) * rows_per_block + row
                slot = jnp.clip(slot_ref[flat], 0, count * cap - 1)
                term = jnp.dot(pool_ref[slot], stencil_ref[member, row],
                               preferred_element_type=jnp.float32)
                total = term if total is None else total + term
            result = total.astype(out_ref.dtype)
            out_ref[:, member * BLK:(member + 1) * BLK] = result
            summed = result.astype(jnp.float32).reshape(bin_count, level_count, BLK).sum(axis=0)
            mean_ref[:, member * BLK:(member + 1) * BLK] = summed / bin_count

    grid_spec = pltpu.PrefetchScalarGridSpec(
        num_scalar_prefetch=1,
        grid=(block_count // group,),
        in_specs=[pl.BlockSpec((group, rows_per_block, BLK, BLK), lambda b, table: (b, 0, 0, 0))]
        + [pl.BlockSpec(memory_space=pl.ANY) for _ in range(count)],
        out_specs=[pl.BlockSpec((rows, group * BLK), lambda b, table: (0, b)),
                   pl.BlockSpec((level_count, group * BLK), lambda b, table: (0, b))],
        scratch_shapes=[pltpu.VMEM((count * cap, rows, BLK), pieces[0].dtype),
                        pltpu.SemaphoreType.DMA((count,))],
    )
    out_shape = [jax.ShapeDtypeStruct((rows, block_count * BLK), pieces[0].dtype),
                 jax.ShapeDtypeStruct((level_count, block_count * BLK), jnp.float32)]
    return pl.pallas_call(
        body, grid_spec=grid_spec, out_shape=out_shape,
        compiler_params=pltpu.CompilerParams(dimension_semantics=("arbitrary",)),
    )(slots, stencil, *pieces)


def shards(
    spectral,
    legendre_value,
    legendre_slope,
    wave_numbers,
    aerosol_old,
    vertical_weight,
    send_blocks,
    depart_slot,
    depart_offset,
    depart_weight,
):
    padded = extended(aerosol_old, (("lev", 1),), 1)
    weights = vertical_weight.astype(jnp.float32)
    vertical_sum = (
        weights[0] * padded[:, :-2] + weights[1] * padded[:, 1:-1] + weights[2] * padded[:, 2:]
    )
    bin_count, level_count, lat_count, lon_count = aerosol_old.shape
    rows = bin_count * level_count
    remapped = vertical_sum.astype(jnp.bfloat16).reshape(rows, lat_count * lon_count)
    block_total = lat_count * lon_count // BLK
    listed = jnp.clip(send_blocks[0], 0, block_total - 1)
    offsets, cap = listed.shape
    outgoing = pack_blocks(listed.reshape(-1), remapped, offsets, cap)
    outgoing, spectral, legendre_value, legendre_slope, depart_offset, depart_weight = (
        lax.optimization_barrier(
            (outgoing, spectral, legendre_value, legendre_slope, depart_offset, depart_weight)
        )
    )
    stencil = stencil_matrix(depart_offset, depart_weight).astype(jnp.bfloat16)
    reach_bands = offsets // 2
    pieces = []
    for offset_index in range(offsets):
        shift_by = offset_index - reach_bands
        if shift_by == 0:
            pieces.append(outgoing[offset_index])
        else:
            pieces.append(shifted(outgoing[offset_index], "band", shift_by))
    band_here = lax.axis_index("band")
    wave_local = spectral.shape[2]
    own_waves = lax.dynamic_slice_in_dim(wave_numbers, band_here * wave_local, wave_local, 0)
    value_terms = jnp.einsum(
        "slj,xksj->xkls", legendre_value, spectral, preferred_element_type=jnp.float32
    )
    slope_terms = jnp.einsum(
        "slj,xksj->xkls", legendre_slope, spectral, preferred_element_type=jnp.float32
    )
    factor = own_waves.astype(jnp.float32) / WAVES
    coefficients = jnp.stack(
        [
            -slope_terms[0] - factor * value_terms[3],
            -slope_terms[1] + factor * value_terms[2],
            slope_terms[2] - factor * value_terms[1],
            slope_terms[3] + factor * value_terms[0],
        ]
    ).astype(jnp.bfloat16)
    received = lax.all_to_all(coefficients, "band", split_axis=2, concat_axis=3, tiled=True)
    wind_grid = synthesis(received, wave_numbers, NLON).astype(jnp.bfloat16)
    flat_new, average = apply_stencil(depart_slot.reshape(-1), stencil, pieces, bin_count, level_count)
    aerosol_new = flat_new.reshape(bin_count, level_count, lat_count, lon_count)
    average = average.reshape(level_count, lat_count, lon_count)
    aerosol_flux = (wind_grid.astype(jnp.float32) * average[None]).astype(jnp.bfloat16)
    return (wind_grid, aerosol_new, aerosol_flux)


def solution(mesh):
    return jax.shard_map(
        shards,
        mesh=mesh,
        in_specs=(
            P(None, "lev", "band", None),
            P("band", None, None),
            P("band", None, None),
            P(),
            P(None, "lev", "band", None),
            P(None, "lev", "band", None),
            P("band", None, None),
            P("band", None),
            P("band", None, None),
            P("band", None, None, None),
        ),
        out_specs=(
            P(None, "lev", "band", None),
            P(None, "lev", "band", None),
            P(None, "lev", "band", None),
        ),
        check_vma=False,
    )
```

```python
import math

import jax
import jax.numpy as jnp
from jax import lax
from jax.experimental import pallas as pl
from jax.experimental.pallas import tpu as pltpu
from jax.sharding import PartitionSpec as P

WAVES = 640
NLON = 2688
BLK = 128


def extended(cells, sides, width):
    for axis, dim in sides:
        count = lax.axis_size(axis)
        ends = count - 1
        head = lax.slice_in_dim(cells, 0, width, axis=dim)
        tail = lax.slice_in_dim(cells, cells.shape[dim] - width, cells.shape[dim], axis=dim)
        cells = jnp.concatenate(
            [
                lax.ppermute(tail, axis, [(i, (i + 1) % count) for i in range(ends)]),
                cells,
                lax.ppermute(head, axis, [((i + 1) % count, i) for i in range(ends)]),
            ],
            axis=dim,
        )
    return cells


def shifted(value, axis, steps):
    count = lax.axis_size(axis)
    leading, last = (max(0, -steps), min(count, count - steps))
    return lax.ppermute(value, axis, [(source, source + steps) for source in range(leading, last)])


def synthesis(coefficients, wave_numbers, lon_count):
    inner = BLK
    outer = lon_count // inner
    waves = wave_numbers[:, None]
    scale = 2.0 * math.pi / lon_count
    near = (waves * jnp.arange(inner, dtype=jnp.int32)[None, :]) % lon_count
    far = (waves * (jnp.arange(outer, dtype=jnp.int32) * inner)[None, :]) % lon_count
    near_angle = near.astype(jnp.float32) * scale
    far_angle = far.astype(jnp.float32) * scale
    doubled = jnp.where(wave_numbers == 0, 1.0, 2.0).astype(jnp.float32)
    far_cos = (doubled[:, None] * jnp.cos(far_angle)).T
    far_sin = (doubled[:, None] * jnp.sin(far_angle)).T
    wide = coefficients.astype(jnp.float32)
    real = wide[0::2][..., None, :]
    imag = wide[1::2][..., None, :]
    first = real * far_cos - imag * far_sin
    second = -(real * far_sin + imag * far_cos)
    lhs = jnp.concatenate([first, second], axis=-1)
    rhs = jnp.concatenate([jnp.cos(near_angle), jnp.sin(near_angle)], axis=0)
    out = jnp.einsum("wklom,mi->wkloi", lhs, rhs, precision=lax.Precision.HIGHEST,
                     preferred_element_type=jnp.float32)
    return out.reshape(out.shape[:3] + (lon_count,))


def stencil_matrix(depart_offset, depart_weight):
    width = depart_offset.shape[-1]
    columns = jnp.arange(width, dtype=jnp.int32)
    summed = jnp.zeros(depart_offset.shape[:2] + (width, width), jnp.float32)
    for term_index in range(depart_weight.shape[2]):
        matches = columns[None, None, :, None] == depart_offset[:, :, None, :] + term_index
        summed = summed + jnp.where(
            matches, depart_weight[:, :, term_index, None, :].astype(jnp.float32), 0.0
        )
    return summed


def pack_blocks(listed, remapped, offsets, cap):
    rows = remapped.shape[0]

    def body(listed_ref, *refs):
        for index in range(offsets):
            refs[offsets + index][...] = refs[index][...][None]

    def source_map(index):
        return lambda entry, table: (0, table[index * cap + entry])

    out_shape = [jax.ShapeDtypeStruct((cap, rows, BLK), remapped.dtype) for _ in range(offsets)]
    grid_spec = pltpu.PrefetchScalarGridSpec(
        num_scalar_prefetch=1,
        grid=(cap,),
        in_specs=[pl.BlockSpec((rows, BLK), source_map(index)) for index in range(offsets)],
        out_specs=[pl.BlockSpec((1, rows, BLK), lambda entry, table: (entry, 0, 0))
                   for _ in range(offsets)],
    )
    return pl.pallas_call(body, grid_spec=grid_spec, out_shape=out_shape)(
        listed, *([remapped] * offsets))


def apply_stencil(slots, stencil, pieces, bin_count, level_count):
    block_count, rows_per_block = stencil.shape[0], stencil.shape[1]
    count = len(pieces)
    cap, rows, _ = pieces[0].shape
    group = 7 if block_count % 7 == 0 else 1

    def body(slot_ref, stencil_ref, *refs):
        piece_refs = refs[:count]
        out_ref, mean_ref, pool_ref, sems = refs[count:]
        block = pl.program_id(0)

        @pl.when(block == 0)
        def _():
            copies = [pltpu.make_async_copy(piece_refs[index], pool_ref.at[pl.ds(index * cap, cap)],
                                            sems.at[index]) for index in range(count)]
            for copy in copies:
                copy.start()
            for copy in copies:
                copy.wait()

        for member in range(group):
            total = None
            for row in range(rows_per_block):
                flat = (block * group + member) * rows_per_block + row
                slot = jnp.clip(slot_ref[flat], 0, count * cap - 1)
                term = jnp.dot(pool_ref[slot], stencil_ref[member, row],
                               preferred_element_type=jnp.float32)
                total = term if total is None else total + term
            result = total.astype(out_ref.dtype)
            out_ref[:, member * BLK:(member + 1) * BLK] = result
            summed = result.astype(jnp.float32).reshape(bin_count, level_count, BLK).sum(axis=0)
            mean_ref[:, member * BLK:(member + 1) * BLK] = summed / bin_count

    grid_spec = pltpu.PrefetchScalarGridSpec(
        num_scalar_prefetch=1,
        grid=(block_count // group,),
        in_specs=[pl.BlockSpec((group, rows_per_block, BLK, BLK), lambda b, table: (b, 0, 0, 0))]
        + [pl.BlockSpec(memory_space=pl.ANY) for _ in range(count)],
        out_specs=[pl.BlockSpec((rows, group * BLK), lambda b, table: (0, b)),
                   pl.BlockSpec((level_count, group * BLK), lambda b, table: (0, b))],
        scratch_shapes=[pltpu.VMEM((count * cap, rows, BLK), pieces[0].dtype),
                        pltpu.SemaphoreType.DMA((count,))],
    )
    out_shape = [jax.ShapeDtypeStruct((rows, block_count * BLK), pieces[0].dtype),
                 jax.ShapeDtypeStruct((level_count, block_count * BLK), jnp.float32)]
    return pl.pallas_call(
        body, grid_spec=grid_spec, out_shape=out_shape,
        compiler_params=pltpu.CompilerParams(dimension_semantics=("arbitrary",)),
    )(slots, stencil, *pieces)


def shards(
    spectral,
    legendre_value,
    legendre_slope,
    wave_numbers,
    aerosol_old,
    vertical_weight,
    send_blocks,
    depart_slot,
    depart_offset,
    depart_weight,
):
    padded = extended(aerosol_old, (("lev", 1),), 1)
    band_here = lax.axis_index("band")
    wave_local = spectral.shape[2]
    own_waves = lax.dynamic_slice_in_dim(wave_numbers, band_here * wave_local, wave_local, 0)
    value_terms = jnp.einsum(
        "slj,xksj->xkls", legendre_value, spectral, preferred_element_type=jnp.float32
    )
    slope_terms = jnp.einsum(
        "slj,xksj->xkls", legendre_slope, spectral, preferred_element_type=jnp.float32
    )
    factor = own_waves.astype(jnp.float32) / WAVES
    coefficients = jnp.stack(
        [
            -slope_terms[0] - factor * value_terms[3],
            -slope_terms[1] + factor * value_terms[2],
            slope_terms[2] - factor * value_terms[1],
            slope_terms[3] + factor * value_terms[0],
        ]
    ).astype(jnp.bfloat16)
    received = lax.all_to_all(coefficients, "band", split_axis=2, concat_axis=3, tiled=True)
    received, padded = lax.optimization_barrier((received, padded))
    weights = vertical_weight.astype(jnp.float32)
    vertical_sum = (
        weights[0] * padded[:, :-2] + weights[1] * padded[:, 1:-1] + weights[2] * padded[:, 2:]
    )
    bin_count, level_count, lat_count, lon_count = aerosol_old.shape
    rows = bin_count * level_count
    remapped = vertical_sum.astype(jnp.bfloat16).reshape(rows, lat_count * lon_count)
    block_total = lat_count * lon_count // BLK
    listed = jnp.clip(send_blocks[0], 0, block_total - 1)
    offsets, cap = listed.shape
    outgoing = pack_blocks(listed.reshape(-1), remapped, offsets, cap)
    outgoing, received, depart_offset, depart_weight = lax.optimization_barrier(
        (outgoing, received, depart_offset, depart_weight)
    )
    stencil = stencil_matrix(depart_offset, depart_weight).astype(jnp.bfloat16)
    reach_bands = offsets // 2
    pieces = []
    for offset_index in range(offsets):
        shift_by = offset_index - reach_bands
        if shift_by == 0:
            pieces.append(outgoing[offset_index])
        else:
            pieces.append(shifted(outgoing[offset_index], "band", shift_by))
    wind_grid = synthesis(received, wave_numbers, NLON).astype(jnp.bfloat16)
    flat_new, average = apply_stencil(depart_slot.reshape(-1), stencil, pieces, bin_count, level_count)
    aerosol_new = flat_new.reshape(bin_count, level_count, lat_count, lon_count)
    average = average.reshape(level_count, lat_count, lon_count)
    aerosol_flux = (wind_grid.astype(jnp.float32) * average[None]).astype(jnp.bfloat16)
    return (wind_grid, aerosol_new, aerosol_flux)


def solution(mesh):
    return jax.shard_map(
        shards,
        mesh=mesh,
        in_specs=(
            P(None, "lev", "band", None),
            P("band", None, None),
            P("band", None, None),
            P(),
            P(None, "lev", "band", None),
            P(None, "lev", "band", None),
            P("band", None, None),
            P("band", None),
            P("band", None, None),
            P("band", None, None, None),
        ),
        out_specs=(
            P(None, "lev", "band", None),
            P(None, "lev", "band", None),
            P(None, "lev", "band", None),
        ),
        check_vma=False,
    )
```

```python
import math

import jax
import jax.numpy as jnp
from jax import lax
from jax.experimental import pallas as pl
from jax.experimental.pallas import tpu as pltpu
from jax.sharding import PartitionSpec as P

WAVES = 640
NLON = 2688
BLK = 128


def extended(cells, sides, width):
    for axis, dim in sides:
        count = lax.axis_size(axis)
        ends = count - 1
        head = lax.slice_in_dim(cells, 0, width, axis=dim)
        tail = lax.slice_in_dim(cells, cells.shape[dim] - width, cells.shape[dim], axis=dim)
        cells = jnp.concatenate(
            [
                lax.ppermute(tail, axis, [(i, (i + 1) % count) for i in range(ends)]),
                cells,
                lax.ppermute(head, axis, [((i + 1) % count, i) for i in range(ends)]),
            ],
            axis=dim,
        )
    return cells


def shifted(value, axis, steps):
    count = lax.axis_size(axis)
    leading, last = (max(0, -steps), min(count, count - steps))
    return lax.ppermute(value, axis, [(source, source + steps) for source in range(leading, last)])


def synthesis(coefficients, wave_numbers, lon_count):
    inner = BLK
    outer = lon_count // inner
    waves = wave_numbers[:, None]
    scale = 2.0 * math.pi / lon_count
    near = (waves * jnp.arange(inner, dtype=jnp.int32)[None, :]) % lon_count
    far = (waves * (jnp.arange(outer, dtype=jnp.int32) * inner)[None, :]) % lon_count
    near_angle = near.astype(jnp.float32) * scale
    far_angle = far.astype(jnp.float32) * scale
    doubled = jnp.where(wave_numbers == 0, 1.0, 2.0).astype(jnp.float32)
    far_cos = (doubled[:, None] * jnp.cos(far_angle)).T
    far_sin = (doubled[:, None] * jnp.sin(far_angle)).T
    wide = coefficients.astype(jnp.float32)
    real = wide[0::2][..., None, :]
    imag = wide[1::2][..., None, :]
    first = real * far_cos - imag * far_sin
    second = -(real * far_sin + imag * far_cos)
    lhs = jnp.concatenate([first, second], axis=-1)
    rhs = jnp.concatenate([jnp.cos(near_angle), jnp.sin(near_angle)], axis=0)
    out = jnp.einsum("wklom,mi->wkloi", lhs, rhs, precision=lax.Precision.HIGHEST,
                     preferred_element_type=jnp.float32)
    return out.reshape(out.shape[:3] + (lon_count,))


def stencil_matrix(depart_offset, depart_weight):
    width = depart_offset.shape[-1]
    columns = jnp.arange(width, dtype=jnp.int32)
    summed = jnp.zeros(depart_offset.shape[:2] + (width, width), jnp.float32)
    for term_index in range(depart_weight.shape[2]):
        matches = columns[None, None, :, None] == depart_offset[:, :, None, :] + term_index
        summed = summed + jnp.where(
            matches, depart_weight[:, :, term_index, None, :].astype(jnp.float32), 0.0
        )
    return summed


def pack_blocks(listed, remapped, offsets, cap):
    rows = remapped.shape[0]

    def body(listed_ref, *refs):
        for index in range(offsets):
            refs[offsets + index][...] = refs[index][...][None]

    def source_map(index):
        return lambda entry, table: (0, table[index * cap + entry])

    out_shape = [jax.ShapeDtypeStruct((cap, rows, BLK), remapped.dtype) for _ in range(offsets)]
    grid_spec = pltpu.PrefetchScalarGridSpec(
        num_scalar_prefetch=1,
        grid=(cap,),
        in_specs=[pl.BlockSpec((rows, BLK), source_map(index)) for index in range(offsets)],
        out_specs=[pl.BlockSpec((1, rows, BLK), lambda entry, table: (entry, 0, 0))
                   for _ in range(offsets)],
    )
    return pl.pallas_call(body, grid_spec=grid_spec, out_shape=out_shape)(
        listed, *([remapped] * offsets))


def apply_stencil(slots, stencil, pieces, bin_count, level_count):
    block_count, rows_per_block = stencil.shape[0], stencil.shape[1]
    count = len(pieces)
    cap, rows, _ = pieces[0].shape
    group = 7 if block_count % 7 == 0 else 1

    def body(slot_ref, stencil_ref, *refs):
        piece_refs = refs[:count]
        out_ref, mean_ref, pool_ref, sems = refs[count:]
        block = pl.program_id(0)

        @pl.when(block == 0)
        def _():
            copies = [pltpu.make_async_copy(piece_refs[index], pool_ref.at[pl.ds(index * cap, cap)],
                                            sems.at[index]) for index in range(count)]
            for copy in copies:
                copy.start()
            for copy in copies:
                copy.wait()

        for member in range(group):
            total = None
            for row in range(rows_per_block):
                flat = (block * group + member) * rows_per_block + row
                slot = jnp.clip(slot_ref[flat], 0, count * cap - 1)
                term = jnp.dot(pool_ref[slot], stencil_ref[member, row],
                               preferred_element_type=jnp.float32)
                total = term if total is None else total + term
            result = total.astype(out_ref.dtype)
            out_ref[:, member * BLK:(member + 1) * BLK] = result
            summed = result.astype(jnp.float32).reshape(bin_count, level_count, BLK).sum(axis=0)
            mean_ref[:, member * BLK:(member + 1) * BLK] = summed / bin_count

    grid_spec = pltpu.PrefetchScalarGridSpec(
        num_scalar_prefetch=1,
        grid=(block_count // group,),
        in_specs=[pl.BlockSpec((group, rows_per_block, BLK, BLK), lambda b, table: (b, 0, 0, 0))]
        + [pl.BlockSpec(memory_space=pl.ANY) for _ in range(count)],
        out_specs=[pl.BlockSpec((rows, group * BLK), lambda b, table: (0, b)),
                   pl.BlockSpec((level_count, group * BLK), lambda b, table: (0, b))],
        scratch_shapes=[pltpu.VMEM((count * cap, rows, BLK), pieces[0].dtype),
                        pltpu.SemaphoreType.DMA((count,))],
    )
    out_shape = [jax.ShapeDtypeStruct((rows, block_count * BLK), pieces[0].dtype),
                 jax.ShapeDtypeStruct((level_count, block_count * BLK), jnp.float32)]
    return pl.pallas_call(
        body, grid_spec=grid_spec, out_shape=out_shape,
        compiler_params=pltpu.CompilerParams(dimension_semantics=("arbitrary",)),
    )(slots, stencil, *pieces)


def shards(
    spectral,
    legendre_value,
    legendre_slope,
    wave_numbers,
    aerosol_old,
    vertical_weight,
    send_blocks,
    depart_slot,
    depart_offset,
    depart_weight,
):
    padded = extended(aerosol_old, (("lev", 1),), 1)
    weights = vertical_weight.astype(jnp.float32)
    vertical_sum = (
        weights[0] * padded[:, :-2] + weights[1] * padded[:, 1:-1] + weights[2] * padded[:, 2:]
    )
    bin_count, level_count, lat_count, lon_count = aerosol_old.shape
    rows = bin_count * level_count
    remapped = vertical_sum.astype(jnp.bfloat16).reshape(rows, lat_count * lon_count)
    block_total = lat_count * lon_count // BLK
    listed = jnp.clip(send_blocks[0], 0, block_total - 1)
    offsets, cap = listed.shape
    outgoing = pack_blocks(listed.reshape(-1), remapped, offsets, cap)
    outgoing, spectral, legendre_value, legendre_slope, depart_offset, depart_weight = (
        lax.optimization_barrier(
            (outgoing, spectral, legendre_value, legendre_slope, depart_offset, depart_weight)
        )
    )
    stencil = stencil_matrix(depart_offset, depart_weight).astype(jnp.bfloat16)
    reach_bands = offsets // 2
    pieces = []
    for offset_index in range(offsets):
        shift_by = offset_index - reach_bands
        if shift_by == 0:
            pieces.append(outgoing[offset_index])
        else:
            pieces.append(shifted(outgoing[offset_index], "band", shift_by))
    band_here = lax.axis_index("band")
    wave_local = spectral.shape[2]
    own_waves = lax.dynamic_slice_in_dim(wave_numbers, band_here * wave_local, wave_local, 0)
    value_terms = jnp.einsum(
        "slj,xksj->xkls", legendre_value, spectral, preferred_element_type=jnp.float32
    )
    slope_terms = jnp.einsum(
        "slj,xksj->xkls", legendre_slope, spectral, preferred_element_type=jnp.float32
    )
    factor = own_waves.astype(jnp.float32) / WAVES
    coefficients = jnp.stack(
        [
            -slope_terms[0] - factor * value_terms[3],
            -slope_terms[1] + factor * value_terms[2],
            slope_terms[2] - factor * value_terms[1],
            slope_terms[3] + factor * value_terms[0],
        ]
    ).astype(jnp.bfloat16)
    received = lax.all_to_all(coefficients, "band", split_axis=2, concat_axis=3, tiled=True)
    wind_grid = synthesis(received, wave_numbers, NLON).astype(jnp.bfloat16)
    flat_new, average = apply_stencil(depart_slot.reshape(-1), stencil, pieces, bin_count, level_count)
    aerosol_new = flat_new.reshape(bin_count, level_count, lat_count, lon_count)
    average = average.reshape(level_count, lat_count, lon_count)
    aerosol_flux = (wind_grid.astype(jnp.float32) * average[None]).astype(jnp.bfloat16)
    return (wind_grid, aerosol_new, aerosol_flux)


def solution(mesh):
    return jax.shard_map(
        shards,
        mesh=mesh,
        in_specs=(
            P(None, "lev", "band", None),
            P("band", None, None),
            P("band", None, None),
            P(),
            P(None, "lev", "band", None),
            P(None, "lev", "band", None),
            P("band", None, None),
            P("band", None),
            P("band", None, None),
            P("band", None, None, None),
        ),
        out_specs=(
            P(None, "lev", "band", None),
            P(None, "lev", "band", None),
            P(None, "lev", "band", None),
        ),
        check_vma=False,
    )
```

```python
import math

import jax
import jax.numpy as jnp
from jax import lax
from jax.experimental import pallas as pl
from jax.experimental.pallas import tpu as pltpu
from jax.sharding import PartitionSpec as P

WAVES = 640
NLON = 2688
BLK = 128


def extended(cells, sides, width):
    for axis, dim in sides:
        count = lax.axis_size(axis)
        ends = count - 1
        head = lax.slice_in_dim(cells, 0, width, axis=dim)
        tail = lax.slice_in_dim(cells, cells.shape[dim] - width, cells.shape[dim], axis=dim)
        cells = jnp.concatenate(
            [
                lax.ppermute(tail, axis, [(i, (i + 1) % count) for i in range(ends)]),
                cells,
                lax.ppermute(head, axis, [((i + 1) % count, i) for i in range(ends)]),
            ],
            axis=dim,
        )
    return cells


def shifted(value, axis, steps):
    count = lax.axis_size(axis)
    leading, last = (max(0, -steps), min(count, count - steps))
    return lax.ppermute(value, axis, [(source, source + steps) for source in range(leading, last)])


def synthesis(coefficients, wave_numbers, lon_count):
    inner = BLK
    outer = lon_count // inner
    waves = wave_numbers[:, None]
    scale = 2.0 * math.pi / lon_count
    near = (waves * jnp.arange(inner, dtype=jnp.int32)[None, :]) % lon_count
    far = (waves * (jnp.arange(outer, dtype=jnp.int32) * inner)[None, :]) % lon_count
    near_angle = near.astype(jnp.float32) * scale
    far_angle = far.astype(jnp.float32) * scale
    doubled = jnp.where(wave_numbers == 0, 1.0, 2.0).astype(jnp.float32)
    far_cos = (doubled[:, None] * jnp.cos(far_angle)).T
    far_sin = (doubled[:, None] * jnp.sin(far_angle)).T
    wide = coefficients.astype(jnp.float32)
    real = wide[0::2][..., None, :]
    imag = wide[1::2][..., None, :]
    first = real * far_cos - imag * far_sin
    second = -(real * far_sin + imag * far_cos)
    lhs = jnp.concatenate([first, second], axis=-1)
    rhs = jnp.concatenate([jnp.cos(near_angle), jnp.sin(near_angle)], axis=0)
    out = jnp.einsum("wklom,mi->wkloi", lhs, rhs, precision=lax.Precision.HIGHEST,
                     preferred_element_type=jnp.float32)
    return out.reshape(out.shape[:3] + (lon_count,))


def stencil_matrix(depart_offset, depart_weight):
    width = depart_offset.shape[-1]
    columns = jnp.arange(width, dtype=jnp.int32)
    summed = jnp.zeros(depart_offset.shape[:2] + (width, width), jnp.float32)
    for term_index in range(depart_weight.shape[2]):
        matches = columns[None, None, :, None] == depart_offset[:, :, None, :] + term_index
        summed = summed + jnp.where(
            matches, depart_weight[:, :, term_index, None, :].astype(jnp.float32), 0.0
        )
    return summed


def pack_blocks(listed, remapped, offsets, cap):
    rows, width = remapped.shape

    def body(listed_ref, source_ref, *out_refs):
        for index in range(offsets):
            for entry in range(cap):
                column = pl.multiple_of(listed_ref[index * cap + entry] * BLK, BLK)
                out_refs[index][entry] = source_ref[:, pl.ds(column, BLK)]

    out_shape = [jax.ShapeDtypeStruct((cap, rows, BLK), remapped.dtype) for _ in range(offsets)]
    grid_spec = pltpu.PrefetchScalarGridSpec(
        num_scalar_prefetch=1,
        grid=(1,),
        in_specs=[pl.BlockSpec((rows, width), lambda step, table: (0, 0))],
        out_specs=[pl.BlockSpec((cap, rows, BLK), lambda step, table: (0, 0, 0))
                   for _ in range(offsets)],
    )
    return pl.pallas_call(body, grid_spec=grid_spec, out_shape=out_shape)(listed, remapped)


def apply_stencil(slots, stencil, pieces, bin_count, level_count):
    block_count, rows_per_block = stencil.shape[0], stencil.shape[1]
    count = len(pieces)
    cap, rows, _ = pieces[0].shape
    group = 7 if block_count % 7 == 0 else 1

    def body(slot_ref, stencil_ref, *refs):
        piece_refs = refs[:count]
        out_ref, mean_ref, pool_ref, sems = refs[count:]
        block = pl.program_id(0)

        @pl.when(block == 0)
        def _():
            copies = [pltpu.make_async_copy(piece_refs[index], pool_ref.at[pl.ds(index * cap, cap)],
                                            sems.at[index]) for index in range(count)]
            for copy in copies:
                copy.start()
            for copy in copies:
                copy.wait()

        for member in range(group):
            total = None
            for row in range(rows_per_block):
                flat = (block * group + member) * rows_per_block + row
                slot = jnp.clip(slot_ref[flat], 0, count * cap - 1)
                term = jnp.dot(pool_ref[slot], stencil_ref[member, row],
                               preferred_element_type=jnp.float32)
                total = term if total is None else total + term
            result = total.astype(out_ref.dtype)
            out_ref[:, member * BLK:(member + 1) * BLK] = result
            summed = result.astype(jnp.float32).reshape(bin_count, level_count, BLK).sum(axis=0)
            mean_ref[:, member * BLK:(member + 1) * BLK] = summed / bin_count

    grid_spec = pltpu.PrefetchScalarGridSpec(
        num_scalar_prefetch=1,
        grid=(block_count // group,),
        in_specs=[pl.BlockSpec((group, rows_per_block, BLK, BLK), lambda b, table: (b, 0, 0, 0))]
        + [pl.BlockSpec(memory_space=pl.ANY) for _ in range(count)],
        out_specs=[pl.BlockSpec((rows, group * BLK), lambda b, table: (0, b)),
                   pl.BlockSpec((level_count, group * BLK), lambda b, table: (0, b))],
        scratch_shapes=[pltpu.VMEM((count * cap, rows, BLK), pieces[0].dtype),
                        pltpu.SemaphoreType.DMA((count,))],
    )
    out_shape = [jax.ShapeDtypeStruct((rows, block_count * BLK), pieces[0].dtype),
                 jax.ShapeDtypeStruct((level_count, block_count * BLK), jnp.float32)]
    return pl.pallas_call(
        body, grid_spec=grid_spec, out_shape=out_shape,
        compiler_params=pltpu.CompilerParams(dimension_semantics=("arbitrary",)),
    )(slots, stencil, *pieces)


def shards(
    spectral,
    legendre_value,
    legendre_slope,
    wave_numbers,
    aerosol_old,
    vertical_weight,
    send_blocks,
    depart_slot,
    depart_offset,
    depart_weight,
):
    padded = extended(aerosol_old, (("lev", 1),), 1)
    weights = vertical_weight.astype(jnp.float32)
    vertical_sum = (
        weights[0] * padded[:, :-2] + weights[1] * padded[:, 1:-1] + weights[2] * padded[:, 2:]
    )
    bin_count, level_count, lat_count, lon_count = aerosol_old.shape
    rows = bin_count * level_count
    remapped = vertical_sum.astype(jnp.bfloat16).reshape(rows, lat_count * lon_count)
    block_total = lat_count * lon_count // BLK
    listed = jnp.clip(send_blocks[0], 0, block_total - 1)
    offsets, cap = listed.shape
    outgoing = pack_blocks(listed.reshape(-1), remapped, offsets, cap)
    outgoing, spectral, legendre_value, legendre_slope, depart_offset, depart_weight = (
        lax.optimization_barrier(
            (outgoing, spectral, legendre_value, legendre_slope, depart_offset, depart_weight)
        )
    )
    stencil = stencil_matrix(depart_offset, depart_weight).astype(jnp.bfloat16)
    reach_bands = offsets // 2
    pieces = []
    for offset_index in range(offsets):
        shift_by = offset_index - reach_bands
        if shift_by == 0:
            pieces.append(outgoing[offset_index])
        else:
            pieces.append(shifted(outgoing[offset_index], "band", shift_by))
    band_here = lax.axis_index("band")
    wave_local = spectral.shape[2]
    own_waves = lax.dynamic_slice_in_dim(wave_numbers, band_here * wave_local, wave_local, 0)
    value_terms = jnp.einsum(
        "slj,xksj->xkls", legendre_value, spectral, preferred_element_type=jnp.float32
    )
    slope_terms = jnp.einsum(
        "slj,xksj->xkls", legendre_slope, spectral, preferred_element_type=jnp.float32
    )
    factor = own_waves.astype(jnp.float32) / WAVES
    coefficients = jnp.stack(
        [
            -slope_terms[0] - factor * value_terms[3],
            -slope_terms[1] + factor * value_terms[2],
            slope_terms[2] - factor * value_terms[1],
            slope_terms[3] + factor * value_terms[0],
        ]
    ).astype(jnp.bfloat16)
    received = lax.all_to_all(coefficients, "band", split_axis=2, concat_axis=3, tiled=True)
    wind_grid = synthesis(received, wave_numbers, NLON).astype(jnp.bfloat16)
    flat_new, average = apply_stencil(depart_slot.reshape(-1), stencil, pieces, bin_count, level_count)
    aerosol_new = flat_new.reshape(bin_count, level_count, lat_count, lon_count)
    average = average.reshape(level_count, lat_count, lon_count)
    aerosol_flux = (wind_grid.astype(jnp.float32) * average[None]).astype(jnp.bfloat16)
    return (wind_grid, aerosol_new, aerosol_flux)


def solution(mesh):
    return jax.shard_map(
        shards,
        mesh=mesh,
        in_specs=(
            P(None, "lev", "band", None),
            P("band", None, None),
            P("band", None, None),
            P(),
            P(None, "lev", "band", None),
            P(None, "lev", "band", None),
            P("band", None, None),
            P("band", None),
            P("band", None, None),
            P("band", None, None, None),
        ),
        out_specs=(
            P(None, "lev", "band", None),
            P(None, "lev", "band", None),
            P(None, "lev", "band", None),
        ),
        check_vma=False,
    )
```

```python
import math

import jax
import jax.numpy as jnp
from jax import lax
from jax.experimental import pallas as pl
from jax.experimental.pallas import tpu as pltpu
from jax.sharding import PartitionSpec as P

WAVES = 640
NLON = 2688
BLK = 128
BAND = ("band_major", "band_minor")
BAND_MINOR = 4


def extended(cells, sides, width):
    for axis, dim in sides:
        count = lax.axis_size(axis)
        ends = count - 1
        head = lax.slice_in_dim(cells, 0, width, axis=dim)
        tail = lax.slice_in_dim(cells, cells.shape[dim] - width, cells.shape[dim], axis=dim)
        cells = jnp.concatenate(
            [
                lax.ppermute(tail, axis, [(i, (i + 1) % count) for i in range(ends)]),
                cells,
                lax.ppermute(head, axis, [((i + 1) % count, i) for i in range(ends)]),
            ],
            axis=dim,
        )
    return cells


def shifted(value, axis, steps):
    count = lax.axis_size(axis[0]) * lax.axis_size(axis[1])
    leading, last = (max(0, -steps), min(count, count - steps))
    return lax.ppermute(value, axis, [(source, source + steps) for source in range(leading, last)])


def synthesis(coefficients, wave_numbers, lon_count):
    inner = BLK
    outer = lon_count // inner
    waves = wave_numbers[:, None]
    scale = 2.0 * math.pi / lon_count
    near = (waves * jnp.arange(inner, dtype=jnp.int32)[None, :]) % lon_count
    far = (waves * (jnp.arange(outer, dtype=jnp.int32) * inner)[None, :]) % lon_count
    near_angle = near.astype(jnp.float32) * scale
    far_angle = far.astype(jnp.float32) * scale
    doubled = jnp.where(wave_numbers == 0, 1.0, 2.0).astype(jnp.float32)
    far_cos = (doubled[:, None] * jnp.cos(far_angle)).T
    far_sin = (doubled[:, None] * jnp.sin(far_angle)).T
    wide = coefficients.astype(jnp.float32)
    real = wide[0::2][..., None, :]
    imag = wide[1::2][..., None, :]
    first = real * far_cos - imag * far_sin
    second = -(real * far_sin + imag * far_cos)
    lhs = jnp.concatenate([first, second], axis=-1)
    rhs = jnp.concatenate([jnp.cos(near_angle), jnp.sin(near_angle)], axis=0)
    out = jnp.einsum("wklom,mi->wkloi", lhs, rhs, precision=lax.Precision.HIGHEST,
                     preferred_element_type=jnp.float32)
    return out.reshape(out.shape[:3] + (lon_count,))


def stencil_matrix(depart_offset, depart_weight):
    width = depart_offset.shape[-1]
    columns = jnp.arange(width, dtype=jnp.int32)
    summed = jnp.zeros(depart_offset.shape[:2] + (width, width), jnp.float32)
    for term_index in range(depart_weight.shape[2]):
        matches = columns[None, None, :, None] == depart_offset[:, :, None, :] + term_index
        summed = summed + jnp.where(
            matches, depart_weight[:, :, term_index, None, :].astype(jnp.float32), 0.0
        )
    return summed


def pack_blocks(listed, remapped, offsets, cap):
    rows, width = remapped.shape

    def body(listed_ref, source_ref, *out_refs):
        for index in range(offsets):
            for entry in range(cap):
                column = pl.multiple_of(listed_ref[index * cap + entry] * BLK, BLK)
                out_refs[index][entry] = source_ref[:, pl.ds(column, BLK)]

    out_shape = [jax.ShapeDtypeStruct((cap, rows, BLK), remapped.dtype) for _ in range(offsets)]
    grid_spec = pltpu.PrefetchScalarGridSpec(
        num_scalar_prefetch=1,
        grid=(1,),
        in_specs=[pl.BlockSpec((rows, width), lambda step, table: (0, 0))],
        out_specs=[pl.BlockSpec((cap, rows, BLK), lambda step, table: (0, 0, 0))
                   for _ in range(offsets)],
    )
    return pl.pallas_call(body, grid_spec=grid_spec, out_shape=out_shape)(listed, remapped)


def apply_stencil(slots, stencil, pieces, bin_count, level_count):
    block_count, rows_per_block = stencil.shape[0], stencil.shape[1]
    count = len(pieces)
    cap, rows, _ = pieces[0].shape
    group = 7 if block_count % 7 == 0 else 1

    def body(slot_ref, stencil_ref, *refs):
        piece_refs = refs[:count]
        out_ref, mean_ref, pool_ref, sems = refs[count:]
        block = pl.program_id(0)

        @pl.when(block == 0)
        def _():
            copies = [pltpu.make_async_copy(piece_refs[index], pool_ref.at[pl.ds(index * cap, cap)],
                                            sems.at[index]) for index in range(count)]
            for copy in copies:
                copy.start()
            for copy in copies:
                copy.wait()

        for member in range(group):
            total = None
            for row in range(rows_per_block):
                flat = (block * group + member) * rows_per_block + row
                slot = jnp.clip(slot_ref[flat], 0, count * cap - 1)
                term = jnp.dot(pool_ref[slot], stencil_ref[member, row],
                               preferred_element_type=jnp.float32)
                total = term if total is None else total + term
            result = total.astype(out_ref.dtype)
            out_ref[:, member * BLK:(member + 1) * BLK] = result
            summed = result.astype(jnp.float32).reshape(bin_count, level_count, BLK).sum(axis=0)
            mean_ref[:, member * BLK:(member + 1) * BLK] = summed / bin_count

    grid_spec = pltpu.PrefetchScalarGridSpec(
        num_scalar_prefetch=1,
        grid=(block_count // group,),
        in_specs=[pl.BlockSpec((group, rows_per_block, BLK, BLK), lambda b, table: (b, 0, 0, 0))]
        + [pl.BlockSpec(memory_space=pl.ANY) for _ in range(count)],
        out_specs=[pl.BlockSpec((rows, group * BLK), lambda b, table: (0, b)),
                   pl.BlockSpec((level_count, group * BLK), lambda b, table: (0, b))],
        scratch_shapes=[pltpu.VMEM((count * cap, rows, BLK), pieces[0].dtype),
                        pltpu.SemaphoreType.DMA((count,))],
    )
    out_shape = [jax.ShapeDtypeStruct((rows, block_count * BLK), pieces[0].dtype),
                 jax.ShapeDtypeStruct((level_count, block_count * BLK), jnp.float32)]
    return pl.pallas_call(
        body, grid_spec=grid_spec, out_shape=out_shape,
        compiler_params=pltpu.CompilerParams(dimension_semantics=("arbitrary",)),
    )(slots, stencil, *pieces)


def shards(
    spectral,
    legendre_value,
    legendre_slope,
    wave_numbers,
    aerosol_old,
    vertical_weight,
    send_blocks,
    depart_slot,
    depart_offset,
    depart_weight,
):
    padded = extended(aerosol_old, (("lev", 1),), 1)
    weights = vertical_weight.astype(jnp.float32)
    vertical_sum = (
        weights[0] * padded[:, :-2] + weights[1] * padded[:, 1:-1] + weights[2] * padded[:, 2:]
    )
    bin_count, level_count, lat_count, lon_count = aerosol_old.shape
    rows = bin_count * level_count
    remapped = vertical_sum.astype(jnp.bfloat16).reshape(rows, lat_count * lon_count)
    block_total = lat_count * lon_count // BLK
    listed = jnp.clip(send_blocks[0], 0, block_total - 1)
    offsets, cap = listed.shape
    outgoing = pack_blocks(listed.reshape(-1), remapped, offsets, cap)
    outgoing, spectral, legendre_value, legendre_slope, depart_offset, depart_weight = (
        lax.optimization_barrier(
            (outgoing, spectral, legendre_value, legendre_slope, depart_offset, depart_weight)
        )
    )
    stencil = stencil_matrix(depart_offset, depart_weight).astype(jnp.bfloat16)
    reach_bands = offsets // 2
    pieces = []
    for offset_index in range(offsets):
        shift_by = offset_index - reach_bands
        if shift_by == 0:
            pieces.append(outgoing[offset_index])
        else:
            pieces.append(shifted(outgoing[offset_index], BAND, shift_by))
    band_here = lax.axis_index(BAND[0]) * lax.axis_size(BAND[1]) + lax.axis_index(BAND[1])
    wave_local = spectral.shape[2]
    own_waves = lax.dynamic_slice_in_dim(wave_numbers, band_here * wave_local, wave_local, 0)
    value_terms = jnp.einsum(
        "slj,xksj->xkls", legendre_value, spectral, preferred_element_type=jnp.float32
    )
    slope_terms = jnp.einsum(
        "slj,xksj->xkls", legendre_slope, spectral, preferred_element_type=jnp.float32
    )
    factor = own_waves.astype(jnp.float32) / WAVES
    coefficients = jnp.stack(
        [
            -slope_terms[0] - factor * value_terms[3],
            -slope_terms[1] + factor * value_terms[2],
            slope_terms[2] - factor * value_terms[1],
            slope_terms[3] + factor * value_terms[0],
        ]
    ).astype(jnp.bfloat16)
    minor = lax.axis_size(BAND[1])
    parts, levels_here, lats, slots = coefficients.shape
    staged = coefficients.reshape(parts, levels_here, lats // minor, minor, slots)
    staged = lax.all_to_all(staged, BAND[1], split_axis=3, concat_axis=4, tiled=True)
    staged = lax.all_to_all(staged, BAND[0], split_axis=2, concat_axis=4, tiled=True)
    received = staged.reshape(parts, levels_here, 1, staged.shape[-1])
    wind_grid = synthesis(received, wave_numbers, NLON).astype(jnp.bfloat16)
    flat_new, average = apply_stencil(depart_slot.reshape(-1), stencil, pieces, bin_count, level_count)
    aerosol_new = flat_new.reshape(bin_count, level_count, lat_count, lon_count)
    average = average.reshape(level_count, lat_count, lon_count)
    aerosol_flux = (wind_grid.astype(jnp.float32) * average[None]).astype(jnp.bfloat16)
    return (wind_grid, aerosol_new, aerosol_flux)


def solution(mesh):
    devices = mesh.devices
    split = jax.sharding.Mesh(
        devices.reshape(devices.shape[0] // BAND_MINOR, BAND_MINOR, devices.shape[1]),
        (BAND[0], BAND[1], mesh.axis_names[1]),
    )
    return jax.shard_map(
        shards,
        mesh=split,
        in_specs=(
            P(None, "lev", BAND, None),
            P(BAND, None, None),
            P(BAND, None, None),
            P(),
            P(None, "lev", BAND, None),
            P(None, "lev", BAND, None),
            P(BAND, None, None),
            P(BAND, None),
            P(BAND, None, None),
            P(BAND, None, None, None),
        ),
        out_specs=(
            P(None, "lev", BAND, None),
            P(None, "lev", BAND, None),
            P(None, "lev", BAND, None),
        ),
        check_vma=False,
    )
```

```python
import math

import jax
import jax.numpy as jnp
from jax import lax
from jax.experimental import pallas as pl
from jax.experimental.pallas import tpu as pltpu
from jax.sharding import PartitionSpec as P

WAVES = 640
NLON = 2688
BLK = 128


def extended(cells, sides, width):
    for axis, dim in sides:
        count = lax.axis_size(axis)
        ends = count - 1
        head = lax.slice_in_dim(cells, 0, width, axis=dim)
        tail = lax.slice_in_dim(cells, cells.shape[dim] - width, cells.shape[dim], axis=dim)
        cells = jnp.concatenate(
            [
                lax.ppermute(tail, axis, [(i, (i + 1) % count) for i in range(ends)]),
                cells,
                lax.ppermute(head, axis, [((i + 1) % count, i) for i in range(ends)]),
            ],
            axis=dim,
        )
    return cells


def shifted(value, axis, steps):
    count = lax.axis_size(axis)
    leading, last = (max(0, -steps), min(count, count - steps))
    return lax.ppermute(value, axis, [(source, source + steps) for source in range(leading, last)])


def synthesis(coefficients, wave_numbers, lon_count):
    inner = BLK
    outer = lon_count // inner
    waves = wave_numbers[:, None]
    scale = 2.0 * math.pi / lon_count
    near = (waves * jnp.arange(inner, dtype=jnp.int32)[None, :]) % lon_count
    far = (waves * (jnp.arange(outer, dtype=jnp.int32) * inner)[None, :]) % lon_count
    near_angle = near.astype(jnp.float32) * scale
    far_angle = far.astype(jnp.float32) * scale
    doubled = jnp.where(wave_numbers == 0, 1.0, 2.0).astype(jnp.float32)
    far_cos = (doubled[:, None] * jnp.cos(far_angle)).T
    far_sin = (doubled[:, None] * jnp.sin(far_angle)).T
    wide = coefficients.astype(jnp.float32)
    real = wide[0::2][..., None, :]
    imag = wide[1::2][..., None, :]
    first = real * far_cos - imag * far_sin
    second = -(real * far_sin + imag * far_cos)
    lhs = jnp.concatenate([first, second], axis=-1)
    rhs = jnp.concatenate([jnp.cos(near_angle), jnp.sin(near_angle)], axis=0)
    out = jnp.einsum("wklom,mi->wkloi", lhs, rhs, precision=lax.Precision.HIGHEST,
                     preferred_element_type=jnp.float32)
    return out.reshape(out.shape[:3] + (lon_count,))


def stencil_matrix(depart_offset, depart_weight):
    width = depart_offset.shape[-1]
    columns = jnp.arange(width, dtype=jnp.int32)
    summed = jnp.zeros(depart_offset.shape[:2] + (width, width), jnp.float32)
    for term_index in range(depart_weight.shape[2]):
        matches = columns[None, None, :, None] == depart_offset[:, :, None, :] + term_index
        summed = summed + jnp.where(
            matches, depart_weight[:, :, term_index, None, :].astype(jnp.float32), 0.0
        )
    return summed


def pack_blocks(listed, remapped, offsets, cap):
    rows, width = remapped.shape

    def body(listed_ref, source_ref, *out_refs):
        for index in range(offsets):
            for entry in range(cap):
                column = pl.multiple_of(listed_ref[index * cap + entry] * BLK, BLK)
                out_refs[index][entry] = source_ref[:, pl.ds(column, BLK)]

    out_shape = [jax.ShapeDtypeStruct((cap, rows, BLK), remapped.dtype) for _ in range(offsets)]
    grid_spec = pltpu.PrefetchScalarGridSpec(
        num_scalar_prefetch=1,
        grid=(1,),
        in_specs=[pl.BlockSpec((rows, width), lambda step, table: (0, 0))],
        out_specs=[pl.BlockSpec((cap, rows, BLK), lambda step, table: (0, 0, 0))
                   for _ in range(offsets)],
    )
    return pl.pallas_call(body, grid_spec=grid_spec, out_shape=out_shape)(listed, remapped)


def apply_stencil(slots, stencil, pieces, bin_count, level_count):
    block_count, rows_per_block = stencil.shape[0], stencil.shape[1]
    count = len(pieces)
    cap, rows, _ = pieces[0].shape
    group = 7 if block_count % 7 == 0 else 1

    def body(slot_ref, stencil_ref, *refs):
        piece_refs = refs[:count]
        out_ref, mean_ref, pool_ref, sems = refs[count:]
        block = pl.program_id(0)

        @pl.when(block == 0)
        def _():
            copies = [pltpu.make_async_copy(piece_refs[index], pool_ref.at[pl.ds(index * cap, cap)],
                                            sems.at[index]) for index in range(count)]
            for copy in copies:
                copy.start()
            for copy in copies:
                copy.wait()

        for member in range(group):
            total = None
            for row in range(rows_per_block):
                flat = (block * group + member) * rows_per_block + row
                slot = jnp.clip(slot_ref[flat], 0, count * cap - 1)
                term = jnp.dot(pool_ref[slot], stencil_ref[member, row],
                               preferred_element_type=jnp.float32)
                total = term if total is None else total + term
            result = total.astype(out_ref.dtype)
            out_ref[:, member * BLK:(member + 1) * BLK] = result
            summed = result.astype(jnp.float32).reshape(bin_count, level_count, BLK).sum(axis=0)
            mean_ref[:, member * BLK:(member + 1) * BLK] = summed / bin_count

    grid_spec = pltpu.PrefetchScalarGridSpec(
        num_scalar_prefetch=1,
        grid=(block_count // group,),
        in_specs=[pl.BlockSpec((group, rows_per_block, BLK, BLK), lambda b, table: (b, 0, 0, 0))]
        + [pl.BlockSpec(memory_space=pl.ANY) for _ in range(count)],
        out_specs=[pl.BlockSpec((rows, group * BLK), lambda b, table: (0, b)),
                   pl.BlockSpec((level_count, group * BLK), lambda b, table: (0, b))],
        scratch_shapes=[pltpu.VMEM((count * cap, rows, BLK), pieces[0].dtype),
                        pltpu.SemaphoreType.DMA((count,))],
    )
    out_shape = [jax.ShapeDtypeStruct((rows, block_count * BLK), pieces[0].dtype),
                 jax.ShapeDtypeStruct((level_count, block_count * BLK), jnp.float32)]
    return pl.pallas_call(
        body, grid_spec=grid_spec, out_shape=out_shape,
        compiler_params=pltpu.CompilerParams(dimension_semantics=("arbitrary",)),
    )(slots, stencil, *pieces)


def shards(
    spectral,
    legendre_value,
    legendre_slope,
    wave_numbers,
    aerosol_old,
    vertical_weight,
    send_blocks,
    depart_slot,
    depart_offset,
    depart_weight,
):
    padded = extended(aerosol_old, (("lev", 1),), 1)
    weights = vertical_weight.astype(jnp.float32)
    vertical_sum = (
        weights[0] * padded[:, :-2] + weights[1] * padded[:, 1:-1] + weights[2] * padded[:, 2:]
    )
    bin_count, level_count, lat_count, lon_count = aerosol_old.shape
    rows = bin_count * level_count
    remapped = vertical_sum.astype(jnp.bfloat16).reshape(rows, lat_count * lon_count)
    block_total = lat_count * lon_count // BLK
    listed = jnp.clip(send_blocks[0], 0, block_total - 1)
    offsets, cap = listed.shape
    outgoing = pack_blocks(listed.reshape(-1), remapped, offsets, cap)
    outgoing, spectral, legendre_value, legendre_slope, depart_offset, depart_weight = (
        lax.optimization_barrier(
            (outgoing, spectral, legendre_value, legendre_slope, depart_offset, depart_weight)
        )
    )
    stencil = stencil_matrix(depart_offset, depart_weight).astype(jnp.bfloat16)
    band_here = lax.axis_index("band")
    wave_local = spectral.shape[2]
    own_waves = lax.dynamic_slice_in_dim(wave_numbers, band_here * wave_local, wave_local, 0)
    value_terms = jnp.einsum(
        "slj,xksj->xkls", legendre_value, spectral, preferred_element_type=jnp.float32
    )
    slope_terms = jnp.einsum(
        "slj,xksj->xkls", legendre_slope, spectral, preferred_element_type=jnp.float32
    )
    factor = own_waves.astype(jnp.float32) / WAVES
    coefficients = jnp.stack(
        [
            -slope_terms[0] - factor * value_terms[3],
            -slope_terms[1] + factor * value_terms[2],
            slope_terms[2] - factor * value_terms[1],
            slope_terms[3] + factor * value_terms[0],
        ]
    ).astype(jnp.bfloat16)
    received = lax.all_to_all(coefficients, "band", split_axis=2, concat_axis=3, tiled=True)
    outgoing, received = lax.optimization_barrier((outgoing, received))
    reach_bands = offsets // 2
    pieces = []
    for offset_index in range(offsets):
        shift_by = offset_index - reach_bands
        if shift_by == 0:
            pieces.append(outgoing[offset_index])
        else:
            pieces.append(shifted(outgoing[offset_index], "band", shift_by))
    wind_grid = synthesis(received, wave_numbers, NLON).astype(jnp.bfloat16)
    flat_new, average = apply_stencil(depart_slot.reshape(-1), stencil, pieces, bin_count, level_count)
    aerosol_new = flat_new.reshape(bin_count, level_count, lat_count, lon_count)
    average = average.reshape(level_count, lat_count, lon_count)
    aerosol_flux = (wind_grid.astype(jnp.float32) * average[None]).astype(jnp.bfloat16)
    return (wind_grid, aerosol_new, aerosol_flux)


def solution(mesh):
    return jax.shard_map(
        shards,
        mesh=mesh,
        in_specs=(
            P(None, "lev", "band", None),
            P("band", None, None),
            P("band", None, None),
            P(),
            P(None, "lev", "band", None),
            P(None, "lev", "band", None),
            P("band", None, None),
            P("band", None),
            P("band", None, None),
            P("band", None, None, None),
        ),
        out_specs=(
            P(None, "lev", "band", None),
            P(None, "lev", "band", None),
            P(None, "lev", "band", None),
        ),
        check_vma=False,
    )
```

```python
import math

import jax
import jax.numpy as jnp
from jax import lax
from jax.experimental import pallas as pl
from jax.experimental.pallas import tpu as pltpu
from jax.sharding import PartitionSpec as P

WAVES = 640
NLON = 2688
BLK = 128


def extended(cells, sides, width):
    for axis, dim in sides:
        count = lax.axis_size(axis)
        ends = count - 1
        head = lax.slice_in_dim(cells, 0, width, axis=dim)
        tail = lax.slice_in_dim(cells, cells.shape[dim] - width, cells.shape[dim], axis=dim)
        cells = jnp.concatenate(
            [
                lax.ppermute(tail, axis, [(i, (i + 1) % count) for i in range(ends)]),
                cells,
                lax.ppermute(head, axis, [((i + 1) % count, i) for i in range(ends)]),
            ],
            axis=dim,
        )
    return cells


def shifted(value, axis, steps):
    count = lax.axis_size(axis)
    leading, last = (max(0, -steps), min(count, count - steps))
    return lax.ppermute(value, axis, [(source, source + steps) for source in range(leading, last)])


def synthesis(coefficients, wave_numbers, lon_count):
    inner = BLK
    outer = lon_count // inner
    waves = wave_numbers[:, None]
    scale = 2.0 * math.pi / lon_count
    near = (waves * jnp.arange(inner, dtype=jnp.int32)[None, :]) % lon_count
    far = (waves * (jnp.arange(outer, dtype=jnp.int32) * inner)[None, :]) % lon_count
    near_angle = near.astype(jnp.float32) * scale
    far_angle = far.astype(jnp.float32) * scale
    doubled = jnp.where(wave_numbers == 0, 1.0, 2.0).astype(jnp.float32)
    far_cos = (doubled[:, None] * jnp.cos(far_angle)).T
    far_sin = (doubled[:, None] * jnp.sin(far_angle)).T
    wide = coefficients.astype(jnp.float32)
    real = wide[0::2][..., None, :]
    imag = wide[1::2][..., None, :]
    first = real * far_cos - imag * far_sin
    second = -(real * far_sin + imag * far_cos)
    lhs = jnp.concatenate([first, second], axis=-1)
    rhs = jnp.concatenate([jnp.cos(near_angle), jnp.sin(near_angle)], axis=0)
    out = jnp.einsum("wklom,mi->wkloi", lhs, rhs, precision=lax.Precision.HIGHEST,
                     preferred_element_type=jnp.float32)
    return out.reshape(out.shape[:3] + (lon_count,))


def stencil_matrix(depart_offset, depart_weight):
    width = depart_offset.shape[-1]
    columns = jnp.arange(width, dtype=jnp.int32)
    summed = jnp.zeros(depart_offset.shape[:2] + (width, width), jnp.float32)
    for term_index in range(depart_weight.shape[2]):
        matches = columns[None, None, :, None] == depart_offset[:, :, None, :] + term_index
        summed = summed + jnp.where(
            matches, depart_weight[:, :, term_index, None, :].astype(jnp.float32), 0.0
        )
    return summed


def pack_blocks(listed, remapped, offsets, cap):
    rows, width = remapped.shape

    def body(listed_ref, source_ref, *out_refs):
        for index in range(offsets):
            for entry in range(cap):
                column = pl.multiple_of(listed_ref[index * cap + entry] * BLK, BLK)
                out_refs[index][entry] = source_ref[:, pl.ds(column, BLK)]

    out_shape = [jax.ShapeDtypeStruct((cap, rows, BLK), remapped.dtype) for _ in range(offsets)]
    grid_spec = pltpu.PrefetchScalarGridSpec(
        num_scalar_prefetch=1,
        grid=(1,),
        in_specs=[pl.BlockSpec((rows, width), lambda step, table: (0, 0))],
        out_specs=[pl.BlockSpec((cap, rows, BLK), lambda step, table: (0, 0, 0))
                   for _ in range(offsets)],
    )
    return pl.pallas_call(body, grid_spec=grid_spec, out_shape=out_shape)(listed, remapped)


def apply_stencil(slots, stencil, pieces, bin_count, level_count):
    block_count, rows_per_block = stencil.shape[0], stencil.shape[1]
    count = len(pieces)
    cap, rows, _ = pieces[0].shape
    group = 7 if block_count % 7 == 0 else 1

    def body(slot_ref, stencil_ref, *refs):
        piece_refs = refs[:count]
        out_ref, mean_ref, pool_ref, sems = refs[count:]
        block = pl.program_id(0)

        @pl.when(block == 0)
        def _():
            copies = [pltpu.make_async_copy(piece_refs[index], pool_ref.at[pl.ds(index * cap, cap)],
                                            sems.at[index]) for index in range(count)]
            for copy in copies:
                copy.start()
            for copy in copies:
                copy.wait()

        for member in range(group):
            total = None
            for row in range(rows_per_block):
                flat = (block * group + member) * rows_per_block + row
                slot = jnp.clip(slot_ref[flat], 0, count * cap - 1)
                term = jnp.dot(pool_ref[slot], stencil_ref[member, row],
                               preferred_element_type=jnp.float32)
                total = term if total is None else total + term
            result = total.astype(out_ref.dtype)
            out_ref[:, member * BLK:(member + 1) * BLK] = result
            summed = result.astype(jnp.float32).reshape(bin_count, level_count, BLK).sum(axis=0)
            mean_ref[:, member * BLK:(member + 1) * BLK] = summed / bin_count

    grid_spec = pltpu.PrefetchScalarGridSpec(
        num_scalar_prefetch=1,
        grid=(block_count // group,),
        in_specs=[pl.BlockSpec((group, rows_per_block, BLK, BLK), lambda b, table: (b, 0, 0, 0))]
        + [pl.BlockSpec(memory_space=pl.ANY) for _ in range(count)],
        out_specs=[pl.BlockSpec((rows, group * BLK), lambda b, table: (0, b)),
                   pl.BlockSpec((level_count, group * BLK), lambda b, table: (0, b))],
        scratch_shapes=[pltpu.VMEM((count * cap, rows, BLK), pieces[0].dtype),
                        pltpu.SemaphoreType.DMA((count,))],
    )
    out_shape = [jax.ShapeDtypeStruct((rows, block_count * BLK), pieces[0].dtype),
                 jax.ShapeDtypeStruct((level_count, block_count * BLK), jnp.float32)]
    return pl.pallas_call(
        body, grid_spec=grid_spec, out_shape=out_shape,
        compiler_params=pltpu.CompilerParams(dimension_semantics=("arbitrary",)),
    )(slots, stencil, *pieces)


def shards(
    spectral,
    legendre_value,
    legendre_slope,
    wave_numbers,
    aerosol_old,
    vertical_weight,
    send_blocks,
    depart_slot,
    depart_offset,
    depart_weight,
):
    padded = extended(aerosol_old, (("lev", 1),), 1)
    weights = vertical_weight.astype(jnp.float32)
    vertical_sum = (
        weights[0] * padded[:, :-2] + weights[1] * padded[:, 1:-1] + weights[2] * padded[:, 2:]
    )
    bin_count, level_count, lat_count, lon_count = aerosol_old.shape
    rows = bin_count * level_count
    remapped = vertical_sum.astype(jnp.bfloat16).reshape(rows, lat_count * lon_count)
    block_total = lat_count * lon_count // BLK
    listed = jnp.clip(send_blocks[0], 0, block_total - 1)
    offsets, cap = listed.shape
    outgoing = pack_blocks(listed.reshape(-1), remapped, offsets, cap)
    gate, spectral, legendre_value, legendre_slope, depart_offset, depart_weight, wave_numbers = (
        lax.optimization_barrier(
            (outgoing, spectral, legendre_value, legendre_slope, depart_offset, depart_weight,
             wave_numbers)
        )
    )
    stencil = stencil_matrix(depart_offset, depart_weight).astype(jnp.bfloat16)
    reach_bands = offsets // 2
    pieces = []
    for offset_index in range(offsets):
        shift_by = offset_index - reach_bands
        if shift_by == 0:
            pieces.append(outgoing[offset_index])
        else:
            pieces.append(shifted(outgoing[offset_index], "band", shift_by))
    band_here = lax.axis_index("band")
    wave_local = spectral.shape[2]
    own_waves = lax.dynamic_slice_in_dim(wave_numbers, band_here * wave_local, wave_local, 0)
    value_terms = jnp.einsum(
        "slj,xksj->xkls", legendre_value, spectral, preferred_element_type=jnp.float32
    )
    slope_terms = jnp.einsum(
        "slj,xksj->xkls", legendre_slope, spectral, preferred_element_type=jnp.float32
    )
    factor = own_waves.astype(jnp.float32) / WAVES
    coefficients = jnp.stack(
        [
            -slope_terms[0] - factor * value_terms[3],
            -slope_terms[1] + factor * value_terms[2],
            slope_terms[2] - factor * value_terms[1],
            slope_terms[3] + factor * value_terms[0],
        ]
    ).astype(jnp.bfloat16)
    received = lax.all_to_all(coefficients, "band", split_axis=2, concat_axis=3, tiled=True)
    wind_grid = synthesis(received, wave_numbers, NLON).astype(jnp.bfloat16)
    flat_new, average = apply_stencil(depart_slot.reshape(-1), stencil, pieces, bin_count, level_count)
    aerosol_new = flat_new.reshape(bin_count, level_count, lat_count, lon_count)
    average = average.reshape(level_count, lat_count, lon_count)
    aerosol_flux = (wind_grid.astype(jnp.float32) * average[None]).astype(jnp.bfloat16)
    return (wind_grid, aerosol_new, aerosol_flux)


def solution(mesh):
    return jax.shard_map(
        shards,
        mesh=mesh,
        in_specs=(
            P(None, "lev", "band", None),
            P("band", None, None),
            P("band", None, None),
            P(),
            P(None, "lev", "band", None),
            P(None, "lev", "band", None),
            P("band", None, None),
            P("band", None),
            P("band", None, None),
            P("band", None, None, None),
        ),
        out_specs=(
            P(None, "lev", "band", None),
            P(None, "lev", "band", None),
            P(None, "lev", "band", None),
        ),
        check_vma=False,
    )
```

```python
import math

import jax
import jax.numpy as jnp
from jax import lax
from jax.experimental import pallas as pl
from jax.experimental.pallas import tpu as pltpu
from jax.sharding import PartitionSpec as P

WAVES = 640
NLON = 2688
BLK = 128


def extended(cells, sides, width):
    for axis, dim in sides:
        count = lax.axis_size(axis)
        ends = count - 1
        head = lax.slice_in_dim(cells, 0, width, axis=dim)
        tail = lax.slice_in_dim(cells, cells.shape[dim] - width, cells.shape[dim], axis=dim)
        cells = jnp.concatenate(
            [
                lax.ppermute(tail, axis, [(i, (i + 1) % count) for i in range(ends)]),
                cells,
                lax.ppermute(head, axis, [((i + 1) % count, i) for i in range(ends)]),
            ],
            axis=dim,
        )
    return cells


def shifted(value, axis, steps):
    count = lax.axis_size(axis)
    leading, last = (max(0, -steps), min(count, count - steps))
    return lax.ppermute(value, axis, [(source, source + steps) for source in range(leading, last)])


def synthesis(coefficients, wave_numbers, lon_count):
    inner = BLK
    outer = lon_count // inner
    waves = wave_numbers[:, None]
    scale = 2.0 * math.pi / lon_count
    near = (waves * jnp.arange(inner, dtype=jnp.int32)[None, :]) % lon_count
    far = (waves * (jnp.arange(outer, dtype=jnp.int32) * inner)[None, :]) % lon_count
    near_angle = near.astype(jnp.float32) * scale
    far_angle = far.astype(jnp.float32) * scale
    doubled = jnp.where(wave_numbers == 0, 1.0, 2.0).astype(jnp.float32)
    far_cos = (doubled[:, None] * jnp.cos(far_angle)).T
    far_sin = (doubled[:, None] * jnp.sin(far_angle)).T
    wide = coefficients.astype(jnp.float32)
    real = wide[0::2][..., None, :]
    imag = wide[1::2][..., None, :]
    first = real * far_cos - imag * far_sin
    second = -(real * far_sin + imag * far_cos)
    lhs = jnp.concatenate([first, second], axis=-1)
    rhs = jnp.concatenate([jnp.cos(near_angle), jnp.sin(near_angle)], axis=0)
    out = jnp.einsum("wklom,mi->wkloi", lhs, rhs, precision=lax.Precision.HIGHEST,
                     preferred_element_type=jnp.float32)
    return out.reshape(out.shape[:3] + (lon_count,))


def stencil_matrix(depart_offset, depart_weight):
    width = depart_offset.shape[-1]
    columns = jnp.arange(width, dtype=jnp.int32)
    summed = jnp.zeros(depart_offset.shape[:2] + (width, width), jnp.float32)
    for term_index in range(depart_weight.shape[2]):
        matches = columns[None, None, :, None] == depart_offset[:, :, None, :] + term_index
        summed = summed + jnp.where(
            matches, depart_weight[:, :, term_index, None, :].astype(jnp.float32), 0.0
        )
    return summed


def pack_blocks(listed, remapped, offsets, cap):
    rows, width = remapped.shape

    def body(listed_ref, source_ref, *out_refs):
        for index in range(offsets):
            for entry in range(cap):
                column = pl.multiple_of(listed_ref[index * cap + entry] * BLK, BLK)
                out_refs[index][entry] = source_ref[:, pl.ds(column, BLK)]

    out_shape = [jax.ShapeDtypeStruct((cap, rows, BLK), remapped.dtype) for _ in range(offsets)]
    grid_spec = pltpu.PrefetchScalarGridSpec(
        num_scalar_prefetch=1,
        grid=(1,),
        in_specs=[pl.BlockSpec((rows, width), lambda step, table: (0, 0))],
        out_specs=[pl.BlockSpec((cap, rows, BLK), lambda step, table: (0, 0, 0))
                   for _ in range(offsets)],
    )
    return pl.pallas_call(body, grid_spec=grid_spec, out_shape=out_shape)(listed, remapped)


def apply_stencil(slots, stencil, pieces, bin_count, level_count):
    block_count, rows_per_block = stencil.shape[0], stencil.shape[1]
    count = len(pieces)
    cap, rows, _ = pieces[0].shape
    group = 7 if block_count % 7 == 0 else 1

    def body(slot_ref, stencil_ref, *refs):
        piece_refs = refs[:count]
        out_ref, mean_ref, pool_ref, sems = refs[count:]
        block = pl.program_id(0)

        @pl.when(block == 0)
        def _():
            copies = [pltpu.make_async_copy(piece_refs[index], pool_ref.at[pl.ds(index * cap, cap)],
                                            sems.at[index]) for index in range(count)]
            for copy in copies:
                copy.start()
            for copy in copies:
                copy.wait()

        for member in range(group):
            total = None
            for row in range(rows_per_block):
                flat = (block * group + member) * rows_per_block + row
                slot = jnp.clip(slot_ref[flat], 0, count * cap - 1)
                term = jnp.dot(pool_ref[slot], stencil_ref[member, row],
                               preferred_element_type=jnp.float32)
                total = term if total is None else total + term
            result = total.astype(out_ref.dtype)
            out_ref[:, member * BLK:(member + 1) * BLK] = result
            summed = result.astype(jnp.float32).reshape(bin_count, level_count, BLK).sum(axis=0)
            mean_ref[:, member * BLK:(member + 1) * BLK] = summed / bin_count

    grid_spec = pltpu.PrefetchScalarGridSpec(
        num_scalar_prefetch=1,
        grid=(block_count // group,),
        in_specs=[pl.BlockSpec((group, rows_per_block, BLK, BLK), lambda b, table: (b, 0, 0, 0))]
        + [pl.BlockSpec(memory_space=pl.ANY) for _ in range(count)],
        out_specs=[pl.BlockSpec((rows, group * BLK), lambda b, table: (0, b)),
                   pl.BlockSpec((level_count, group * BLK), lambda b, table: (0, b))],
        scratch_shapes=[pltpu.VMEM((count * cap, rows, BLK), pieces[0].dtype),
                        pltpu.SemaphoreType.DMA((count,))],
    )
    out_shape = [jax.ShapeDtypeStruct((rows, block_count * BLK), pieces[0].dtype),
                 jax.ShapeDtypeStruct((level_count, block_count * BLK), jnp.float32)]
    return pl.pallas_call(
        body, grid_spec=grid_spec, out_shape=out_shape,
        compiler_params=pltpu.CompilerParams(dimension_semantics=("arbitrary",)),
    )(slots, stencil, *pieces)


def shards(
    spectral,
    legendre_value,
    legendre_slope,
    wave_numbers,
    aerosol_old,
    vertical_weight,
    send_blocks,
    depart_slot,
    depart_offset,
    depart_weight,
):
    band_here = lax.axis_index("band")
    wave_local = spectral.shape[2]
    own_waves = lax.dynamic_slice_in_dim(wave_numbers, band_here * wave_local, wave_local, 0)
    value_terms = jnp.einsum(
        "slj,xksj->xkls", legendre_value, spectral, preferred_element_type=jnp.float32
    )
    slope_terms = jnp.einsum(
        "slj,xksj->xkls", legendre_slope, spectral, preferred_element_type=jnp.float32
    )
    factor = own_waves.astype(jnp.float32) / WAVES
    coefficients = jnp.stack(
        [
            -slope_terms[0] - factor * value_terms[3],
            -slope_terms[1] + factor * value_terms[2],
            slope_terms[2] - factor * value_terms[1],
            slope_terms[3] + factor * value_terms[0],
        ]
    ).astype(jnp.bfloat16)
    padded = extended(aerosol_old, (("lev", 1),), 1)
    weights = vertical_weight.astype(jnp.float32)
    vertical_sum = (
        weights[0] * padded[:, :-2] + weights[1] * padded[:, 1:-1] + weights[2] * padded[:, 2:]
    )
    bin_count, level_count, lat_count, lon_count = aerosol_old.shape
    rows = bin_count * level_count
    remapped = vertical_sum.astype(jnp.bfloat16).reshape(rows, lat_count * lon_count)
    block_total = lat_count * lon_count // BLK
    listed = jnp.clip(send_blocks[0], 0, block_total - 1)
    offsets, cap = listed.shape
    outgoing = pack_blocks(listed.reshape(-1), remapped, offsets, cap)
    gate, coefficients, depart_offset, depart_weight, wave_numbers = lax.optimization_barrier(
        (outgoing, coefficients, depart_offset, depart_weight, wave_numbers)
    )
    stencil = stencil_matrix(depart_offset, depart_weight).astype(jnp.bfloat16)
    reach_bands = offsets // 2
    pieces = []
    for offset_index in range(offsets):
        shift_by = offset_index - reach_bands
        if shift_by == 0:
            pieces.append(outgoing[offset_index])
        else:
            pieces.append(shifted(outgoing[offset_index], "band", shift_by))
    received = lax.all_to_all(coefficients, "band", split_axis=2, concat_axis=3, tiled=True)
    wind_grid = synthesis(received, wave_numbers, NLON).astype(jnp.bfloat16)
    flat_new, average = apply_stencil(depart_slot.reshape(-1), stencil, pieces, bin_count, level_count)
    aerosol_new = flat_new.reshape(bin_count, level_count, lat_count, lon_count)
    average = average.reshape(level_count, lat_count, lon_count)
    aerosol_flux = (wind_grid.astype(jnp.float32) * average[None]).astype(jnp.bfloat16)
    return (wind_grid, aerosol_new, aerosol_flux)


def solution(mesh):
    return jax.shard_map(
        shards,
        mesh=mesh,
        in_specs=(
            P(None, "lev", "band", None),
            P("band", None, None),
            P("band", None, None),
            P(),
            P(None, "lev", "band", None),
            P(None, "lev", "band", None),
            P("band", None, None),
            P("band", None),
            P("band", None, None),
            P("band", None, None, None),
        ),
        out_specs=(
            P(None, "lev", "band", None),
            P(None, "lev", "band", None),
            P(None, "lev", "band", None),
        ),
        check_vma=False,
    )
```

```python
import math

import jax
import jax.numpy as jnp
from jax import lax
from jax.experimental import pallas as pl
from jax.experimental.pallas import tpu as pltpu
from jax.sharding import PartitionSpec as P

WAVES = 640
NLON = 2688
BLK = 128


def extended(cells, sides, width):
    for axis, dim in sides:
        count = lax.axis_size(axis)
        ends = count - 1
        head = lax.slice_in_dim(cells, 0, width, axis=dim)
        tail = lax.slice_in_dim(cells, cells.shape[dim] - width, cells.shape[dim], axis=dim)
        cells = jnp.concatenate(
            [
                lax.ppermute(tail, axis, [(i, (i + 1) % count) for i in range(ends)]),
                cells,
                lax.ppermute(head, axis, [((i + 1) % count, i) for i in range(ends)]),
            ],
            axis=dim,
        )
    return cells


def shifted(value, axis, steps):
    count = lax.axis_size(axis)
    leading, last = (max(0, -steps), min(count, count - steps))
    return lax.ppermute(value, axis, [(source, source + steps) for source in range(leading, last)])


def synthesis(coefficients, wave_numbers, lon_count):
    inner = BLK
    outer = lon_count // inner
    waves = wave_numbers[:, None]
    scale = 2.0 * math.pi / lon_count
    near = (waves * jnp.arange(inner, dtype=jnp.int32)[None, :]) % lon_count
    far = (waves * (jnp.arange(outer, dtype=jnp.int32) * inner)[None, :]) % lon_count
    near_angle = near.astype(jnp.float32) * scale
    far_angle = far.astype(jnp.float32) * scale
    doubled = jnp.where(wave_numbers == 0, 1.0, 2.0).astype(jnp.float32)
    far_cos = (doubled[:, None] * jnp.cos(far_angle)).T
    far_sin = (doubled[:, None] * jnp.sin(far_angle)).T
    wide = coefficients.astype(jnp.float32)
    real = wide[0::2][..., None, :]
    imag = wide[1::2][..., None, :]
    first = real * far_cos - imag * far_sin
    second = -(real * far_sin + imag * far_cos)
    lhs = jnp.concatenate([first, second], axis=-1)
    rhs = jnp.concatenate([jnp.cos(near_angle), jnp.sin(near_angle)], axis=0)
    out = jnp.einsum("wklom,mi->wkloi", lhs, rhs, precision=lax.Precision.HIGHEST,
                     preferred_element_type=jnp.float32)
    return out.reshape(out.shape[:3] + (lon_count,))


def stencil_matrix(depart_offset, depart_weight):
    width = depart_offset.shape[-1]
    columns = jnp.arange(width, dtype=jnp.int32)
    summed = jnp.zeros(depart_offset.shape[:2] + (width, width), jnp.float32)
    for term_index in range(depart_weight.shape[2]):
        matches = columns[None, None, :, None] == depart_offset[:, :, None, :] + term_index
        summed = summed + jnp.where(
            matches, depart_weight[:, :, term_index, None, :].astype(jnp.float32), 0.0
        )
    return summed


def pack_blocks(listed, remapped, offsets, cap):
    rows, width = remapped.shape

    def body(listed_ref, source_ref, *out_refs):
        for index in range(offsets):
            for entry in range(cap):
                column = pl.multiple_of(listed_ref[index * cap + entry] * BLK, BLK)
                out_refs[index][entry] = source_ref[:, pl.ds(column, BLK)]

    out_shape = [jax.ShapeDtypeStruct((cap, rows, BLK), remapped.dtype) for _ in range(offsets)]
    grid_spec = pltpu.PrefetchScalarGridSpec(
        num_scalar_prefetch=1,
        grid=(1,),
        in_specs=[pl.BlockSpec((rows, width), lambda step, table: (0, 0))],
        out_specs=[pl.BlockSpec((cap, rows, BLK), lambda step, table: (0, 0, 0))
                   for _ in range(offsets)],
    )
    return pl.pallas_call(body, grid_spec=grid_spec, out_shape=out_shape)(listed, remapped)


def apply_stencil(slots, stencil, pieces, bin_count, level_count):
    block_count, rows_per_block = stencil.shape[0], stencil.shape[1]
    count = len(pieces)
    cap, rows, _ = pieces[0].shape
    group = 7 if block_count % 7 == 0 else 1

    def body(slot_ref, stencil_ref, *refs):
        piece_refs = refs[:count]
        out_ref, mean_ref, pool_ref, sems = refs[count:]
        block = pl.program_id(0)

        @pl.when(block == 0)
        def _():
            copies = [pltpu.make_async_copy(piece_refs[index], pool_ref.at[pl.ds(index * cap, cap)],
                                            sems.at[index]) for index in range(count)]
            for copy in copies:
                copy.start()
            for copy in copies:
                copy.wait()

        for member in range(group):
            total = None
            for row in range(rows_per_block):
                flat = (block * group + member) * rows_per_block + row
                slot = jnp.clip(slot_ref[flat], 0, count * cap - 1)
                term = jnp.dot(pool_ref[slot], stencil_ref[member, row],
                               preferred_element_type=jnp.float32)
                total = term if total is None else total + term
            result = total.astype(out_ref.dtype)
            out_ref[:, member * BLK:(member + 1) * BLK] = result
            summed = result.astype(jnp.float32).reshape(bin_count, level_count, BLK).sum(axis=0)
            mean_ref[:, member * BLK:(member + 1) * BLK] = summed / bin_count

    grid_spec = pltpu.PrefetchScalarGridSpec(
        num_scalar_prefetch=1,
        grid=(block_count // group,),
        in_specs=[pl.BlockSpec((group, rows_per_block, BLK, BLK), lambda b, table: (b, 0, 0, 0))]
        + [pl.BlockSpec(memory_space=pl.ANY) for _ in range(count)],
        out_specs=[pl.BlockSpec((rows, group * BLK), lambda b, table: (0, b)),
                   pl.BlockSpec((level_count, group * BLK), lambda b, table: (0, b))],
        scratch_shapes=[pltpu.VMEM((count * cap, rows, BLK), pieces[0].dtype),
                        pltpu.SemaphoreType.DMA((count,))],
    )
    out_shape = [jax.ShapeDtypeStruct((rows, block_count * BLK), pieces[0].dtype),
                 jax.ShapeDtypeStruct((level_count, block_count * BLK), jnp.float32)]
    return pl.pallas_call(
        body, grid_spec=grid_spec, out_shape=out_shape,
        compiler_params=pltpu.CompilerParams(dimension_semantics=("arbitrary",)),
    )(slots, stencil, *pieces)


def shards(
    spectral,
    legendre_value,
    legendre_slope,
    wave_numbers,
    aerosol_old,
    vertical_weight,
    send_blocks,
    depart_slot,
    depart_offset,
    depart_weight,
):
    padded = extended(aerosol_old, (("lev", 1),), 1)
    weights = vertical_weight.astype(jnp.float32)
    vertical_sum = (
        weights[0] * padded[:, :-2] + weights[1] * padded[:, 1:-1] + weights[2] * padded[:, 2:]
    )
    bin_count, level_count, lat_count, lon_count = aerosol_old.shape
    rows = bin_count * level_count
    remapped = vertical_sum.astype(jnp.bfloat16).reshape(rows, lat_count * lon_count)
    block_total = lat_count * lon_count // BLK
    listed = jnp.clip(send_blocks[0], 0, block_total - 1)
    offsets, cap = listed.shape
    outgoing = pack_blocks(listed.reshape(-1), remapped, offsets, cap)
    gate, spectral, legendre_value, legendre_slope, depart_offset, depart_weight, wave_numbers = (
        lax.optimization_barrier(
            (outgoing, spectral, legendre_value, legendre_slope, depart_offset, depart_weight,
             wave_numbers)
        )
    )
    stencil = stencil_matrix(depart_offset, depart_weight).astype(jnp.bfloat16)
    reach_bands = offsets // 2
    pieces = [None] * offsets
    for offset_index in range(offsets):
        shift_by = offset_index - reach_bands
        if shift_by == 0:
            pieces[offset_index] = outgoing[offset_index]
        elif abs(shift_by) == 1:
            pieces[offset_index] = shifted(outgoing[offset_index], "band", shift_by)
    band_here = lax.axis_index("band")
    wave_local = spectral.shape[2]
    own_waves = lax.dynamic_slice_in_dim(wave_numbers, band_here * wave_local, wave_local, 0)
    value_terms = jnp.einsum(
        "slj,xksj->xkls", legendre_value, spectral, preferred_element_type=jnp.float32
    )
    slope_terms = jnp.einsum(
        "slj,xksj->xkls", legendre_slope, spectral, preferred_element_type=jnp.float32
    )
    factor = own_waves.astype(jnp.float32) / WAVES
    coefficients = jnp.stack(
        [
            -slope_terms[0] - factor * value_terms[3],
            -slope_terms[1] + factor * value_terms[2],
            slope_terms[2] - factor * value_terms[1],
            slope_terms[3] + factor * value_terms[0],
        ]
    ).astype(jnp.bfloat16)
    received = lax.all_to_all(coefficients, "band", split_axis=2, concat_axis=3, tiled=True)
    far = [index for index in range(offsets) if abs(index - reach_bands) > 1]
    late, received = lax.optimization_barrier(([outgoing[index] for index in far], received))
    for index, value in zip(far, late):
        pieces[index] = shifted(value, "band", index - reach_bands)
    wind_grid = synthesis(received, wave_numbers, NLON).astype(jnp.bfloat16)
    flat_new, average = apply_stencil(depart_slot.reshape(-1), stencil, pieces, bin_count, level_count)
    aerosol_new = flat_new.reshape(bin_count, level_count, lat_count, lon_count)
    average = average.reshape(level_count, lat_count, lon_count)
    aerosol_flux = (wind_grid.astype(jnp.float32) * average[None]).astype(jnp.bfloat16)
    return (wind_grid, aerosol_new, aerosol_flux)


def solution(mesh):
    return jax.shard_map(
        shards,
        mesh=mesh,
        in_specs=(
            P(None, "lev", "band", None),
            P("band", None, None),
            P("band", None, None),
            P(),
            P(None, "lev", "band", None),
            P(None, "lev", "band", None),
            P("band", None, None),
            P("band", None),
            P("band", None, None),
            P("band", None, None, None),
        ),
        out_specs=(
            P(None, "lev", "band", None),
            P(None, "lev", "band", None),
            P(None, "lev", "band", None),
        ),
        check_vma=False,
    )
```

```python
import math

import jax
import jax.numpy as jnp
from jax import lax
from jax.experimental import pallas as pl
from jax.experimental.pallas import tpu as pltpu
from jax.sharding import PartitionSpec as P

WAVES = 640
NLON = 2688
BLK = 128


def extended(cells, sides, width):
    for axis, dim in sides:
        count = lax.axis_size(axis)
        ends = count - 1
        head = lax.slice_in_dim(cells, 0, width, axis=dim)
        tail = lax.slice_in_dim(cells, cells.shape[dim] - width, cells.shape[dim], axis=dim)
        cells = jnp.concatenate(
            [
                lax.ppermute(tail, axis, [(i, (i + 1) % count) for i in range(ends)]),
                cells,
                lax.ppermute(head, axis, [((i + 1) % count, i) for i in range(ends)]),
            ],
            axis=dim,
        )
    return cells


def shifted(value, axis, steps):
    count = lax.axis_size(axis)
    leading, last = (max(0, -steps), min(count, count - steps))
    return lax.ppermute(value, axis, [(source, source + steps) for source in range(leading, last)])


def synthesis(coefficients, wave_numbers, lon_count):
    inner = BLK
    outer = lon_count // inner
    waves = wave_numbers[:, None]
    scale = 2.0 * math.pi / lon_count
    near = (waves * jnp.arange(inner, dtype=jnp.int32)[None, :]) % lon_count
    far = (waves * (jnp.arange(outer, dtype=jnp.int32) * inner)[None, :]) % lon_count
    near_angle = near.astype(jnp.float32) * scale
    far_angle = far.astype(jnp.float32) * scale
    doubled = jnp.where(wave_numbers == 0, 1.0, 2.0).astype(jnp.float32)
    far_cos = (doubled[:, None] * jnp.cos(far_angle)).T
    far_sin = (doubled[:, None] * jnp.sin(far_angle)).T
    wide = coefficients.astype(jnp.float32)
    real = wide[0::2][..., None, :]
    imag = wide[1::2][..., None, :]
    first = real * far_cos - imag * far_sin
    second = -(real * far_sin + imag * far_cos)
    lhs = jnp.concatenate([first, second], axis=-1)
    rhs = jnp.concatenate([jnp.cos(near_angle), jnp.sin(near_angle)], axis=0)
    out = jnp.einsum("wklom,mi->wkloi", lhs, rhs, precision=lax.Precision.HIGHEST,
                     preferred_element_type=jnp.float32)
    return out.reshape(out.shape[:3] + (lon_count,))


def stencil_matrix(depart_offset, depart_weight):
    width = depart_offset.shape[-1]
    columns = jnp.arange(width, dtype=jnp.int32)
    summed = jnp.zeros(depart_offset.shape[:2] + (width, width), jnp.float32)
    for term_index in range(depart_weight.shape[2]):
        matches = columns[None, None, :, None] == depart_offset[:, :, None, :] + term_index
        summed = summed + jnp.where(
            matches, depart_weight[:, :, term_index, None, :].astype(jnp.float32), 0.0
        )
    return summed


def pack_blocks(listed, remapped, offsets, cap):
    rows, width = remapped.shape

    def body(listed_ref, source_ref, *out_refs):
        for index in range(offsets):
            for entry in range(cap):
                column = pl.multiple_of(listed_ref[index * cap + entry] * BLK, BLK)
                out_refs[index][entry] = source_ref[:, pl.ds(column, BLK)]

    out_shape = [jax.ShapeDtypeStruct((cap, rows, BLK), remapped.dtype) for _ in range(offsets)]
    grid_spec = pltpu.PrefetchScalarGridSpec(
        num_scalar_prefetch=1,
        grid=(1,),
        in_specs=[pl.BlockSpec((rows, width), lambda step, table: (0, 0))],
        out_specs=[pl.BlockSpec((cap, rows, BLK), lambda step, table: (0, 0, 0))
                   for _ in range(offsets)],
    )
    return pl.pallas_call(body, grid_spec=grid_spec, out_shape=out_shape)(listed, remapped)


def apply_stencil(slots, stencil, pieces, wind, bin_count, level_count):
    block_count, rows_per_block = stencil.shape[0], stencil.shape[1]
    count = len(pieces)
    cap, rows, _ = pieces[0].shape
    group = 7 if block_count % 7 == 0 else 1

    def body(slot_ref, stencil_ref, wind_ref, *refs):
        piece_refs = refs[:count]
        out_ref, flux_ref, pool_ref, sems = refs[count:]
        block = pl.program_id(0)

        @pl.when(block == 0)
        def _():
            copies = [pltpu.make_async_copy(piece_refs[index], pool_ref.at[pl.ds(index * cap, cap)],
                                            sems.at[index]) for index in range(count)]
            for copy in copies:
                copy.start()
            for copy in copies:
                copy.wait()

        for member in range(group):
            total = None
            for row in range(rows_per_block):
                flat = (block * group + member) * rows_per_block + row
                slot = jnp.clip(slot_ref[flat], 0, count * cap - 1)
                term = jnp.dot(pool_ref[slot], stencil_ref[member, row],
                               preferred_element_type=jnp.float32)
                total = term if total is None else total + term
            result = total.astype(out_ref.dtype)
            out_ref[:, member * BLK:(member + 1) * BLK] = result
            summed = result.astype(jnp.float32).reshape(bin_count, level_count, BLK).sum(axis=0)
            average = summed / bin_count
            for part in range(wind_ref.shape[0]):
                wide = wind_ref[part, :, member * BLK:(member + 1) * BLK].astype(jnp.float32)
                flux_ref[part, :, member * BLK:(member + 1) * BLK] = (wide * average).astype(
                    flux_ref.dtype)

    grid_spec = pltpu.PrefetchScalarGridSpec(
        num_scalar_prefetch=1,
        grid=(block_count // group,),
        in_specs=[pl.BlockSpec((group, rows_per_block, BLK, BLK), lambda b, table: (b, 0, 0, 0)),
                  pl.BlockSpec((wind.shape[0], level_count, group * BLK), lambda b, table: (0, 0, b))]
        + [pl.BlockSpec(memory_space=pl.ANY) for _ in range(count)],
        out_specs=[pl.BlockSpec((rows, group * BLK), lambda b, table: (0, b)),
                   pl.BlockSpec((wind.shape[0], level_count, group * BLK),
                                lambda b, table: (0, 0, b))],
        scratch_shapes=[pltpu.VMEM((count * cap, rows, BLK), pieces[0].dtype),
                        pltpu.SemaphoreType.DMA((count,))],
    )
    out_shape = [jax.ShapeDtypeStruct((rows, block_count * BLK), pieces[0].dtype),
                 jax.ShapeDtypeStruct(wind.shape, wind.dtype)]
    return pl.pallas_call(
        body, grid_spec=grid_spec, out_shape=out_shape,
        compiler_params=pltpu.CompilerParams(dimension_semantics=("arbitrary",)),
    )(slots, stencil, wind, *pieces)


def shards(
    spectral,
    legendre_value,
    legendre_slope,
    wave_numbers,
    aerosol_old,
    vertical_weight,
    send_blocks,
    depart_slot,
    depart_offset,
    depart_weight,
):
    padded = extended(aerosol_old, (("lev", 1),), 1)
    weights = vertical_weight.astype(jnp.float32)
    vertical_sum = (
        weights[0] * padded[:, :-2] + weights[1] * padded[:, 1:-1] + weights[2] * padded[:, 2:]
    )
    bin_count, level_count, lat_count, lon_count = aerosol_old.shape
    rows = bin_count * level_count
    remapped = vertical_sum.astype(jnp.bfloat16).reshape(rows, lat_count * lon_count)
    block_total = lat_count * lon_count // BLK
    listed = jnp.clip(send_blocks[0], 0, block_total - 1)
    offsets, cap = listed.shape
    outgoing = pack_blocks(listed.reshape(-1), remapped, offsets, cap)
    gate, spectral, legendre_value, legendre_slope, depart_offset, depart_weight, wave_numbers = (
        lax.optimization_barrier(
            (outgoing, spectral, legendre_value, legendre_slope, depart_offset, depart_weight,
             wave_numbers)
        )
    )
    stencil = stencil_matrix(depart_offset, depart_weight).astype(jnp.bfloat16)
    reach_bands = offsets // 2
    pieces = []
    for offset_index in range(offsets):
        shift_by = offset_index - reach_bands
        if shift_by == 0:
            pieces.append(outgoing[offset_index])
        else:
            pieces.append(shifted(outgoing[offset_index], "band", shift_by))
    band_here = lax.axis_index("band")
    wave_local = spectral.shape[2]
    own_waves = lax.dynamic_slice_in_dim(wave_numbers, band_here * wave_local, wave_local, 0)
    value_terms = jnp.einsum(
        "slj,xksj->xkls", legendre_value, spectral, preferred_element_type=jnp.float32
    )
    slope_terms = jnp.einsum(
        "slj,xksj->xkls", legendre_slope, spectral, preferred_element_type=jnp.float32
    )
    factor = own_waves.astype(jnp.float32) / WAVES
    coefficients = jnp.stack(
        [
            -slope_terms[0] - factor * value_terms[3],
            -slope_terms[1] + factor * value_terms[2],
            slope_terms[2] - factor * value_terms[1],
            slope_terms[3] + factor * value_terms[0],
        ]
    ).astype(jnp.bfloat16)
    received = lax.all_to_all(coefficients, "band", split_axis=2, concat_axis=3, tiled=True)
    wind_grid = synthesis(received, wave_numbers, NLON).astype(jnp.bfloat16)
    wind_rows = wind_grid.reshape(wind_grid.shape[0], level_count, lat_count * lon_count)
    flat_new, flux_rows = apply_stencil(depart_slot.reshape(-1), stencil, pieces, wind_rows,
                                        bin_count, level_count)
    aerosol_new = flat_new.reshape(bin_count, level_count, lat_count, lon_count)
    aerosol_flux = flux_rows.reshape(wind_grid.shape)
    return (wind_grid, aerosol_new, aerosol_flux)


def solution(mesh):
    return jax.shard_map(
        shards,
        mesh=mesh,
        in_specs=(
            P(None, "lev", "band", None),
            P("band", None, None),
            P("band", None, None),
            P(),
            P(None, "lev", "band", None),
            P(None, "lev", "band", None),
            P("band", None, None),
            P("band", None),
            P("band", None, None),
            P("band", None, None, None),
        ),
        out_specs=(
            P(None, "lev", "band", None),
            P(None, "lev", "band", None),
            P(None, "lev", "band", None),
        ),
        check_vma=False,
    )
```

```python
import math

import jax
import jax.numpy as jnp
from jax import lax
from jax.experimental import pallas as pl
from jax.experimental.pallas import tpu as pltpu
from jax.sharding import PartitionSpec as P

WAVES = 640
NLON = 2688
BLK = 128


def extended(cells, sides, width):
    for axis, dim in sides:
        count = lax.axis_size(axis)
        ends = count - 1
        head = lax.slice_in_dim(cells, 0, width, axis=dim)
        tail = lax.slice_in_dim(cells, cells.shape[dim] - width, cells.shape[dim], axis=dim)
        cells = jnp.concatenate(
            [
                lax.ppermute(tail, axis, [(i, (i + 1) % count) for i in range(ends)]),
                cells,
                lax.ppermute(head, axis, [((i + 1) % count, i) for i in range(ends)]),
            ],
            axis=dim,
        )
    return cells


def shifted(value, axis, steps):
    count = lax.axis_size(axis)
    leading, last = (max(0, -steps), min(count, count - steps))
    return lax.ppermute(value, axis, [(source, source + steps) for source in range(leading, last)])


def synthesis(coefficients, wave_numbers, lon_count):
    inner = BLK
    outer = lon_count // inner
    waves = wave_numbers[:, None]
    scale = 2.0 * math.pi / lon_count
    near = (waves * jnp.arange(inner, dtype=jnp.int32)[None, :]) % lon_count
    far = (waves * (jnp.arange(outer, dtype=jnp.int32) * inner)[None, :]) % lon_count
    near_angle = near.astype(jnp.float32) * scale
    far_angle = far.astype(jnp.float32) * scale
    doubled = jnp.where(wave_numbers == 0, 1.0, 2.0).astype(jnp.float32)
    far_cos = (doubled[:, None] * jnp.cos(far_angle)).T
    far_sin = (doubled[:, None] * jnp.sin(far_angle)).T
    wide = coefficients.astype(jnp.float32)
    real = wide[0::2][..., None, :]
    imag = wide[1::2][..., None, :]
    first = real * far_cos - imag * far_sin
    second = -(real * far_sin + imag * far_cos)
    lhs = jnp.concatenate([first, second], axis=-1)
    rhs = jnp.concatenate([jnp.cos(near_angle), jnp.sin(near_angle)], axis=0)
    out = jnp.einsum("wklom,mi->wkloi", lhs, rhs, precision=lax.Precision.HIGHEST,
                     preferred_element_type=jnp.float32)
    return out.reshape(out.shape[:3] + (lon_count,))


def stencil_matrix(depart_offset, depart_weight):
    width = depart_offset.shape[-1]
    columns = jnp.arange(width, dtype=jnp.int32)
    summed = jnp.zeros(depart_offset.shape[:2] + (width, width), jnp.float32)
    for term_index in range(depart_weight.shape[2]):
        matches = columns[None, None, :, None] == depart_offset[:, :, None, :] + term_index
        summed = summed + jnp.where(
            matches, depart_weight[:, :, term_index, None, :].astype(jnp.float32), 0.0
        )
    return summed


def pack_blocks(listed, remapped, offsets, cap):
    rows, width = remapped.shape

    def body(listed_ref, source_ref, *out_refs):
        for index in range(offsets):
            for entry in range(cap):
                column = pl.multiple_of(listed_ref[index * cap + entry] * BLK, BLK)
                out_refs[index][entry] = source_ref[:, pl.ds(column, BLK)]

    out_shape = [jax.ShapeDtypeStruct((cap, rows, BLK), remapped.dtype) for _ in range(offsets)]
    grid_spec = pltpu.PrefetchScalarGridSpec(
        num_scalar_prefetch=1,
        grid=(1,),
        in_specs=[pl.BlockSpec((rows, width), lambda step, table: (0, 0))],
        out_specs=[pl.BlockSpec((cap, rows, BLK), lambda step, table: (0, 0, 0))
                   for _ in range(offsets)],
    )
    return pl.pallas_call(body, grid_spec=grid_spec, out_shape=out_shape)(listed, remapped)


def apply_stencil(slots, stencil, pieces, bin_count, level_count):
    block_count, rows_per_block = stencil.shape[0], stencil.shape[1]
    count = len(pieces)
    cap, rows, _ = pieces[0].shape
    group = block_count

    def body(slot_ref, stencil_ref, *refs):
        piece_refs = refs[:count]
        out_ref, mean_ref, pool_ref, sems = refs[count:]
        block = pl.program_id(0)

        @pl.when(block == 0)
        def _():
            copies = [pltpu.make_async_copy(piece_refs[index], pool_ref.at[pl.ds(index * cap, cap)],
                                            sems.at[index]) for index in range(count)]
            for copy in copies:
                copy.start()
            for copy in copies:
                copy.wait()

        for member in range(group):
            total = None
            for row in range(rows_per_block):
                flat = (block * group + member) * rows_per_block + row
                slot = jnp.clip(slot_ref[flat], 0, count * cap - 1)
                term = jnp.dot(pool_ref[slot], stencil_ref[member, row],
                               preferred_element_type=jnp.float32)
                total = term if total is None else total + term
            result = total.astype(out_ref.dtype)
            out_ref[:, member * BLK:(member + 1) * BLK] = result
            summed = result.astype(jnp.float32).reshape(bin_count, level_count, BLK).sum(axis=0)
            mean_ref[:, member * BLK:(member + 1) * BLK] = summed / bin_count

    grid_spec = pltpu.PrefetchScalarGridSpec(
        num_scalar_prefetch=1,
        grid=(block_count // group,),
        in_specs=[pl.BlockSpec((group, rows_per_block, BLK, BLK), lambda b, table: (b, 0, 0, 0))]
        + [pl.BlockSpec(memory_space=pl.ANY) for _ in range(count)],
        out_specs=[pl.BlockSpec((rows, group * BLK), lambda b, table: (0, b)),
                   pl.BlockSpec((level_count, group * BLK), lambda b, table: (0, b))],
        scratch_shapes=[pltpu.VMEM((count * cap, rows, BLK), pieces[0].dtype),
                        pltpu.SemaphoreType.DMA((count,))],
    )
    out_shape = [jax.ShapeDtypeStruct((rows, block_count * BLK), pieces[0].dtype),
                 jax.ShapeDtypeStruct((level_count, block_count * BLK), jnp.float32)]
    return pl.pallas_call(
        body, grid_spec=grid_spec, out_shape=out_shape,
        compiler_params=pltpu.CompilerParams(dimension_semantics=("arbitrary",)),
    )(slots, stencil, *pieces)


def shards(
    spectral,
    legendre_value,
    legendre_slope,
    wave_numbers,
    aerosol_old,
    vertical_weight,
    send_blocks,
    depart_slot,
    depart_offset,
    depart_weight,
):
    padded = extended(aerosol_old, (("lev", 1),), 1)
    weights = vertical_weight.astype(jnp.float32)
    vertical_sum = (
        weights[0] * padded[:, :-2] + weights[1] * padded[:, 1:-1] + weights[2] * padded[:, 2:]
    )
    bin_count, level_count, lat_count, lon_count = aerosol_old.shape
    rows = bin_count * level_count
    remapped = vertical_sum.astype(jnp.bfloat16).reshape(rows, lat_count * lon_count)
    block_total = lat_count * lon_count // BLK
    listed = jnp.clip(send_blocks[0], 0, block_total - 1)
    offsets, cap = listed.shape
    outgoing = pack_blocks(listed.reshape(-1), remapped, offsets, cap)
    gate, spectral, legendre_value, legendre_slope, depart_offset, depart_weight, wave_numbers = (
        lax.optimization_barrier(
            (outgoing, spectral, legendre_value, legendre_slope, depart_offset, depart_weight,
             wave_numbers)
        )
    )
    stencil = stencil_matrix(depart_offset, depart_weight).astype(jnp.bfloat16)
    reach_bands = offsets // 2
    pieces = []
    for offset_index in range(offsets):
        shift_by = offset_index - reach_bands
        if shift_by == 0:
            pieces.append(outgoing[offset_index])
        else:
            pieces.append(shifted(outgoing[offset_index], "band", shift_by))
    band_here = lax.axis_index("band")
    wave_local = spectral.shape[2]
    own_waves = lax.dynamic_slice_in_dim(wave_numbers, band_here * wave_local, wave_local, 0)
    value_terms = jnp.einsum(
        "slj,xksj->xkls", legendre_value, spectral, preferred_element_type=jnp.float32
    )
    slope_terms = jnp.einsum(
        "slj,xksj->xkls", legendre_slope, spectral, preferred_element_type=jnp.float32
    )
    factor = own_waves.astype(jnp.float32) / WAVES
    coefficients = jnp.stack(
        [
            -slope_terms[0] - factor * value_terms[3],
            -slope_terms[1] + factor * value_terms[2],
            slope_terms[2] - factor * value_terms[1],
            slope_terms[3] + factor * value_terms[0],
        ]
    ).astype(jnp.bfloat16)
    received = lax.all_to_all(coefficients, "band", split_axis=2, concat_axis=3, tiled=True)
    wind_grid = synthesis(received, wave_numbers, NLON).astype(jnp.bfloat16)
    flat_new, average = apply_stencil(depart_slot.reshape(-1), stencil, pieces, bin_count, level_count)
    aerosol_new = flat_new.reshape(bin_count, level_count, lat_count, lon_count)
    average = average.reshape(level_count, lat_count, lon_count)
    aerosol_flux = (wind_grid.astype(jnp.float32) * average[None]).astype(jnp.bfloat16)
    return (wind_grid, aerosol_new, aerosol_flux)


def solution(mesh):
    return jax.shard_map(
        shards,
        mesh=mesh,
        in_specs=(
            P(None, "lev", "band", None),
            P("band", None, None),
            P("band", None, None),
            P(),
            P(None, "lev", "band", None),
            P(None, "lev", "band", None),
            P("band", None, None),
            P("band", None),
            P("band", None, None),
            P("band", None, None, None),
        ),
        out_specs=(
            P(None, "lev", "band", None),
            P(None, "lev", "band", None),
            P(None, "lev", "band", None),
        ),
        check_vma=False,
    )
```

```python
import math

import jax
import jax.numpy as jnp
from jax import lax
from jax.experimental import pallas as pl
from jax.experimental.pallas import tpu as pltpu
from jax.sharding import PartitionSpec as P

WAVES = 640
NLON = 2688
BLK = 128


def extended(cells, sides, width):
    for axis, dim in sides:
        count = lax.axis_size(axis)
        ends = count - 1
        head = lax.slice_in_dim(cells, 0, width, axis=dim)
        tail = lax.slice_in_dim(cells, cells.shape[dim] - width, cells.shape[dim], axis=dim)
        cells = jnp.concatenate(
            [
                lax.ppermute(tail, axis, [(i, (i + 1) % count) for i in range(ends)]),
                cells,
                lax.ppermute(head, axis, [((i + 1) % count, i) for i in range(ends)]),
            ],
            axis=dim,
        )
    return cells


def shifted(value, axis, steps):
    count = lax.axis_size(axis)
    leading, last = (max(0, -steps), min(count, count - steps))
    return lax.ppermute(value, axis, [(source, source + steps) for source in range(leading, last)])


def synthesis(coefficients, wave_numbers, lon_count):
    inner = BLK
    outer = lon_count // inner
    waves = wave_numbers[:, None]
    scale = 2.0 * math.pi / lon_count
    near = (waves * jnp.arange(inner, dtype=jnp.int32)[None, :]) % lon_count
    far = (waves * (jnp.arange(outer, dtype=jnp.int32) * inner)[None, :]) % lon_count
    near_angle = near.astype(jnp.float32) * scale
    far_angle = far.astype(jnp.float32) * scale
    doubled = jnp.where(wave_numbers == 0, 1.0, 2.0).astype(jnp.float32)
    far_cos = (doubled[:, None] * jnp.cos(far_angle)).T
    far_sin = (doubled[:, None] * jnp.sin(far_angle)).T
    wide = coefficients.astype(jnp.float32)
    real = wide[0::2][..., None, :]
    imag = wide[1::2][..., None, :]
    first = real * far_cos - imag * far_sin
    second = -(real * far_sin + imag * far_cos)
    lhs = jnp.concatenate([first, second], axis=-1)
    rhs = jnp.concatenate([jnp.cos(near_angle), jnp.sin(near_angle)], axis=0)
    out = jnp.einsum("wklom,mi->wkloi", lhs, rhs, precision=lax.Precision.HIGHEST,
                     preferred_element_type=jnp.float32)
    return out.reshape(out.shape[:3] + (lon_count,))


def stencil_matrix(depart_offset, depart_weight):
    width = depart_offset.shape[-1]
    columns = jnp.arange(width, dtype=jnp.int32)
    summed = jnp.zeros(depart_offset.shape[:2] + (width, width), jnp.float32)
    for term_index in range(depart_weight.shape[2]):
        matches = columns[None, None, :, None] == depart_offset[:, :, None, :] + term_index
        summed = summed + jnp.where(
            matches, depart_weight[:, :, term_index, None, :].astype(jnp.float32), 0.0
        )
    return summed


def pack_blocks(listed, remapped, offsets, cap):
    rows, width = remapped.shape

    def body(listed_ref, source_ref, *out_refs):
        for index in range(offsets):
            for entry in range(cap):
                column = pl.multiple_of(listed_ref[index * cap + entry] * BLK, BLK)
                out_refs[index][entry] = source_ref[:, pl.ds(column, BLK)]

    out_shape = [jax.ShapeDtypeStruct((cap, rows, BLK), remapped.dtype) for _ in range(offsets)]
    grid_spec = pltpu.PrefetchScalarGridSpec(
        num_scalar_prefetch=1,
        grid=(1,),
        in_specs=[pl.BlockSpec((rows, width), lambda step, table: (0, 0))],
        out_specs=[pl.BlockSpec((cap, rows, BLK), lambda step, table: (0, 0, 0))
                   for _ in range(offsets)],
    )
    return pl.pallas_call(body, grid_spec=grid_spec, out_shape=out_shape)(listed, remapped)


def apply_stencil(slots, stencil, pieces, wind, bin_count, level_count):
    block_count, rows_per_block = stencil.shape[0], stencil.shape[1]
    count = len(pieces)
    cap, rows, _ = pieces[0].shape
    group = block_count

    def body(slot_ref, stencil_ref, wind_ref, *refs):
        piece_refs = refs[:count]
        out_ref, flux_ref, pool_ref, sems = refs[count:]
        block = pl.program_id(0)

        @pl.when(block == 0)
        def _():
            copies = [pltpu.make_async_copy(piece_refs[index], pool_ref.at[pl.ds(index * cap, cap)],
                                            sems.at[index]) for index in range(count)]
            for copy in copies:
                copy.start()
            for copy in copies:
                copy.wait()

        for member in range(group):
            total = None
            for row in range(rows_per_block):
                flat = (block * group + member) * rows_per_block + row
                slot = jnp.clip(slot_ref[flat], 0, count * cap - 1)
                term = jnp.dot(pool_ref[slot], stencil_ref[member, row],
                               preferred_element_type=jnp.float32)
                total = term if total is None else total + term
            result = total.astype(out_ref.dtype)
            out_ref[:, member * BLK:(member + 1) * BLK] = result
            summed = result.astype(jnp.float32).reshape(bin_count, level_count, BLK).sum(axis=0)
            average = summed / bin_count
            for part in range(wind_ref.shape[0]):
                wide = wind_ref[part, :, member * BLK:(member + 1) * BLK].astype(jnp.float32)
                flux_ref[part, :, member * BLK:(member + 1) * BLK] = (wide * average).astype(
                    flux_ref.dtype)

    grid_spec = pltpu.PrefetchScalarGridSpec(
        num_scalar_prefetch=1,
        grid=(block_count // group,),
        in_specs=[pl.BlockSpec((group, rows_per_block, BLK, BLK), lambda b, table: (b, 0, 0, 0)),
                  pl.BlockSpec((wind.shape[0], level_count, group * BLK), lambda b, table: (0, 0, b))]
        + [pl.BlockSpec(memory_space=pl.ANY) for _ in range(count)],
        out_specs=[pl.BlockSpec((rows, group * BLK), lambda b, table: (0, b)),
                   pl.BlockSpec((wind.shape[0], level_count, group * BLK),
                                lambda b, table: (0, 0, b))],
        scratch_shapes=[pltpu.VMEM((count * cap, rows, BLK), pieces[0].dtype),
                        pltpu.SemaphoreType.DMA((count,))],
    )
    out_shape = [jax.ShapeDtypeStruct((rows, block_count * BLK), pieces[0].dtype),
                 jax.ShapeDtypeStruct(wind.shape, wind.dtype)]
    return pl.pallas_call(
        body, grid_spec=grid_spec, out_shape=out_shape,
        compiler_params=pltpu.CompilerParams(dimension_semantics=("arbitrary",)),
    )(slots, stencil, wind, *pieces)


def shards(
    spectral,
    legendre_value,
    legendre_slope,
    wave_numbers,
    aerosol_old,
    vertical_weight,
    send_blocks,
    depart_slot,
    depart_offset,
    depart_weight,
):
    padded = extended(aerosol_old, (("lev", 1),), 1)
    weights = vertical_weight.astype(jnp.float32)
    vertical_sum = (
        weights[0] * padded[:, :-2] + weights[1] * padded[:, 1:-1] + weights[2] * padded[:, 2:]
    )
    bin_count, level_count, lat_count, lon_count = aerosol_old.shape
    rows = bin_count * level_count
    remapped = vertical_sum.astype(jnp.bfloat16).reshape(rows, lat_count * lon_count)
    block_total = lat_count * lon_count // BLK
    listed = jnp.clip(send_blocks[0], 0, block_total - 1)
    offsets, cap = listed.shape
    outgoing = pack_blocks(listed.reshape(-1), remapped, offsets, cap)
    gate, spectral, legendre_value, legendre_slope, depart_offset, depart_weight, wave_numbers = (
        lax.optimization_barrier(
            (outgoing, spectral, legendre_value, legendre_slope, depart_offset, depart_weight,
             wave_numbers)
        )
    )
    stencil = stencil_matrix(depart_offset, depart_weight).astype(jnp.bfloat16)
    reach_bands = offsets // 2
    pieces = []
    for offset_index in range(offsets):
        shift_by = offset_index - reach_bands
        if shift_by == 0:
            pieces.append(outgoing[offset_index])
        else:
            pieces.append(shifted(outgoing[offset_index], "band", shift_by))
    band_here = lax.axis_index("band")
    wave_local = spectral.shape[2]
    own_waves = lax.dynamic_slice_in_dim(wave_numbers, band_here * wave_local, wave_local, 0)
    value_terms = jnp.einsum(
        "slj,xksj->xkls", legendre_value, spectral, preferred_element_type=jnp.float32
    )
    slope_terms = jnp.einsum(
        "slj,xksj->xkls", legendre_slope, spectral, preferred_element_type=jnp.float32
    )
    factor = own_waves.astype(jnp.float32) / WAVES
    coefficients = jnp.stack(
        [
            -slope_terms[0] - factor * value_terms[3],
            -slope_terms[1] + factor * value_terms[2],
            slope_terms[2] - factor * value_terms[1],
            slope_terms[3] + factor * value_terms[0],
        ]
    ).astype(jnp.bfloat16)
    received = lax.all_to_all(coefficients, "band", split_axis=2, concat_axis=3, tiled=True)
    wind_grid = synthesis(received, wave_numbers, NLON).astype(jnp.bfloat16)
    wind_rows = wind_grid.reshape(wind_grid.shape[0], level_count, lat_count * lon_count)
    flat_new, flux_rows = apply_stencil(depart_slot.reshape(-1), stencil, pieces, wind_rows,
                                        bin_count, level_count)
    aerosol_new = flat_new.reshape(bin_count, level_count, lat_count, lon_count)
    aerosol_flux = flux_rows.reshape(wind_grid.shape)
    return (wind_grid, aerosol_new, aerosol_flux)


def solution(mesh):
    return jax.shard_map(
        shards,
        mesh=mesh,
        in_specs=(
            P(None, "lev", "band", None),
            P("band", None, None),
            P("band", None, None),
            P(),
            P(None, "lev", "band", None),
            P(None, "lev", "band", None),
            P("band", None, None),
            P("band", None),
            P("band", None, None),
            P("band", None, None, None),
        ),
        out_specs=(
            P(None, "lev", "band", None),
            P(None, "lev", "band", None),
            P(None, "lev", "band", None),
        ),
        check_vma=False,
    )
```
